32 devices in a mesh: parts: 2 (over x), seq: 16 (over z, y, core).
Axes of the slice: x: 2, y: 2, z: 4, core: 2. Of those that a mesh axis runs over, the one named last changes fastest.
Arguments:
- queries: bfloat16 [4096, 2048], P(('parts', 'seq')), parts along dimension 0
- joined_keys_values: bfloat16 [4096, 2048], P(('parts', 'seq')), parts along dimension 0
- segment_ids: int32 [4096], P(('parts', 'seq')), parts along dimension 0, may hold values from 0 to 3, never falling along the last dimension, each value on 1 to 1024 neighbouring positions
- residual: bfloat16 [4096, 2688], P(('parts', 'seq')), parts along dimension 0, may hold values from -4 to 4
- norm_gain: float32 [2688], replicated, may hold values from 0.5 to 1.5
- out_proj: bfloat16 [2048, 2688], P('seq'), may hold values from -1 to 1
- head_weight: bfloat16 [16384, 2688], P('seq')
- next_ids: int32 [128], P('parts'), parts along dimension 0, may hold values from 0 to 16383
Outputs:
- layer_out: bfloat16 [4096, 2688], P(('parts', 'seq')), parts along dimension 0
- log_probs: float32 [128, 16384], P('parts', 'seq'), parts along dimension 0
- target_logp: float32 [128], P(('parts', 'seq')), parts along dimension 0
The draws below stay inside these ranges and needn't reach their ends.
There are 2 independent parts, one for each index of `parts`. The reference program is written for one: setup_inputs(seed, part) draws one part's arguments, and reference() takes and returns one part's arrays. A program takes and returns all parts, laid end to end along the dimension named above; an argument that names none is the same for every part. Nothing has to cross between parts.
All inputs are finite; a program needn't handle non-finite values.
Results may differ from the reference program's by a relative error of at most 0.0056.
Values may be sent and summed in bfloat16 or wider, within the bound.
No kernel may reach another device: no remote copies, remote signals or barrier semaphores. Data moves between devices by JAX's collectives and lax.ppermute only.
A program may use at most 64 MiB of HBM per device.

```python
import math
import jax
import jax.numpy as jnp
import numpy as np
from jax import lax

D = 2688
QUERY_HEADS = 16
KEY_VALUE_HEADS = 8
HEAD_SIZE = 128
ATTENTION_SPAN = 1024
DOCS = 4
SCORE_DEV = 4
TOK_DEV = 128
SEQUENCE_TOKENS = 2048
VOCAB = 16384
SCORED = 64


def draw_queries(key, part):
    array_shape = (SEQUENCE_TOKENS, QUERY_HEADS * HEAD_SIZE)
    inner_key = jax.random.fold_in(key, 21)
    drawn = jnp.clip(jax.random.normal(inner_key, array_shape, jnp.float32), -6.0, 6.0)
    return drawn.astype(jnp.bfloat16)


def draw_joined_keys_values(key, part):
    array_shape = (SEQUENCE_TOKENS, 2 * KEY_VALUE_HEADS * HEAD_SIZE)
    inner_key = jax.random.fold_in(key, 22)
    drawn = jnp.clip(jax.random.normal(inner_key, array_shape, jnp.float32), -6.0, 6.0)
    return drawn.astype(jnp.bfloat16)


def draw_head_weight(key, part):
    array_shape = (VOCAB, D)
    inner_key = jax.random.fold_in(key, 31)
    spread = math.sqrt(12.0 / D)
    drawn = jnp.clip(jax.random.normal(inner_key, array_shape, jnp.float32), -6.0, 6.0) * spread
    return drawn.astype(jnp.bfloat16)


def place_ends(result, key, least, top_value):
    extent = result.shape
    place = [jax.random.randint(jax.random.fold_in(key, axis), (), 0, extent[axis]) for axis in range(len(extent))]
    result = result.at[tuple(place)].set(least)
    longest = extent.index(max(extent))
    place[longest] = (place[longest] + 1) % extent[longest]
    return result.at[tuple(place)].set(top_value)


def block_levels(rng, extent, shards, low, largest):
    factor_of = 1.0
    for position, parts in shards:
        steps = jax.random.uniform(jax.random.fold_in(jax.random.fold_in(rng, 6), position), (parts,), jnp.float32, low / len(shards), largest / len(shards))
        factor_of = factor_of * jnp.repeat(jnp.exp(steps), extent[position] // parts).reshape((-1,) + (1,) * (len(extent) - 1 - position))
    return factor_of


def cumulative_ranks(amount, skew):
    weights = [(1 << 20) // math.isqrt(rank ** skew) + 1 for rank in range(1, amount + 1)]
    deviation = 1 + sum(weights) // (1 << 30)
    return np.cumsum(np.array([max(1, weight // deviation) for weight in weights]))


def ranked(own_key, shape, number_of, lean):
    listing = cumulative_ranks(number_of, lean)
    pick = jax.random.randint(jax.random.fold_in(own_key, 1), shape, 0, int(listing[number_of - 1]))
    standing = jnp.searchsorted(jnp.asarray(listing, jnp.int32), pick, side="right")
    return jax.random.permutation(jax.random.fold_in(own_key, 2), number_of)[standing].astype(jnp.int32)


def split_up(amount, total, limit, skew):
    portions = [(1 << 20) // math.isqrt(rank ** skew) + 1 for rank in range(2, amount + 1)]
    surplus, counts = total - limit - (amount - 1), [1] * (amount - 1)
    while surplus > 0:
        movable = [i for i in range(amount - 1) if counts[i] < limit]
        whole, left = sum([portions[i] for i in movable]), surplus
        for i in movable:
            extra = min(limit - counts[i], max(1, left * portions[i] // whole), surplus)
            counts[i] = counts[i] + extra
            surplus = surplus - extra
    return np.array([limit] + counts)


def uneven(rng, number_of, total, reach, skew):
    if number_of == 2:
        one = jax.random.randint(rng, (), max(1, total - reach), min(reach, total - 1) + 1)
        return jnp.stack([one, total - one])
    lengths = jnp.asarray(split_up(number_of, total, reach, skew), jnp.int32)
    couples = (number_of - 1) // 2
    source_of, receiver = lengths[1:1 + 2 * couples:2], lengths[2:2 + 2 * couples:2]
    slack = jnp.minimum(source_of - 1, reach - receiver)
    passed = jax.random.randint(jax.random.fold_in(rng, 1), (couples,), 0, 1 << 20) % (slack + 1)
    lengths = lengths.at[1:1 + 2 * couples:2].set(source_of - passed).at[2:2 + 2 * couples:2].set(receiver + passed)
    return lengths[jax.random.permutation(jax.random.fold_in(rng, 2), number_of)]


def noise(own_key, shape, scale, most, cuts=(), kind=jnp.bfloat16):
    loudness = block_levels(own_key, shape, cuts, -0.22, 0.18) if cuts else 1.0
    values = jax.random.normal(own_key, shape, jnp.float32) * scale * loudness
    return jnp.minimum(jnp.maximum(values, -most), most).astype(kind)


def setup_inputs(seed: int = 0, part: int = 0) -> dict:
    seeds = jax.random.split(jax.random.key(seed), 9)
    part_keys = jax.random.split(jax.random.fold_in(seeds[8], part), 9)
    return {
        "queries": draw_queries(jax.random.fold_in(jax.random.fold_in(seeds[8], part), 71), part),
        "joined_keys_values": draw_joined_keys_values(jax.random.fold_in(jax.random.fold_in(seeds[8], part), 71), part),
        "segment_ids": jnp.searchsorted(jnp.cumsum(uneven(part_keys[2], DOCS, SEQUENCE_TOKENS, SEQUENCE_TOKENS // 2, 0)), jnp.arange(SEQUENCE_TOKENS), side="right").astype(jnp.int32),
        "residual": noise(part_keys[3], (SEQUENCE_TOKENS, D), 0.3, 4.0, ((0, 16),)),
        "norm_gain": jnp.clip(1.0 + 0.1 * jax.random.normal(seeds[4], (D,), jnp.float32), 0.5, 1.5),
        "out_proj": noise(seeds[5], (QUERY_HEADS * HEAD_SIZE, D), (QUERY_HEADS * HEAD_SIZE // 64) ** -0.5, 1.0, ((0, 16),)),
        "head_weight": draw_head_weight(jax.random.fold_in(seeds[8], 71), part),
        "next_ids": place_ends(ranked(part_keys[7], (SCORED,), VOCAB, 2), jax.random.fold_in(part_keys[7], 3), 0, VOCAB - 1).astype(jnp.int32),
    }


score_scale = 168.0 ** (-0.5)
masked_score = -1e+30

def reference(queries, joined_keys_values, segment_ids, residual, norm_gain, out_proj, head_weight, next_ids):
    queries_per_group = QUERY_HEADS // KEY_VALUE_HEADS
    stride = TOK_DEV // SCORE_DEV
    rows_per_block = 512 if SEQUENCE_TOKENS % 512 == 0 else SEQUENCE_TOKENS
    block_count = SEQUENCE_TOKENS // rows_per_block
    padded_key_values = jnp.concatenate([jnp.zeros((ATTENTION_SPAN, 2 * KEY_VALUE_HEADS * HEAD_SIZE), jnp.bfloat16), joined_keys_values], 0)
    padded_seg = jnp.concatenate([jnp.full((ATTENTION_SPAN,), -1, jnp.int32), segment_ids.astype(jnp.int32)], 0)

    def attend(block_index):
        offset = (block_index * rows_per_block).astype(jnp.int32)
        rows_of_queries = lax.dynamic_slice_in_dim(queries, offset, rows_per_block, 0)
        heads_for_queries = rows_of_queries.reshape(rows_per_block, KEY_VALUE_HEADS, queries_per_group, HEAD_SIZE).astype(jnp.float32)
        key_value_pair = lax.dynamic_slice_in_dim(padded_key_values, offset, rows_per_block + ATTENTION_SPAN, 0)
        heads_for_keys = key_value_pair[:, :KEY_VALUE_HEADS * HEAD_SIZE].reshape(rows_per_block + ATTENTION_SPAN, KEY_VALUE_HEADS, HEAD_SIZE).astype(jnp.float32)
        heads_for_values = key_value_pair[:, KEY_VALUE_HEADS * HEAD_SIZE:].reshape(rows_per_block + ATTENTION_SPAN, KEY_VALUE_HEADS, HEAD_SIZE).astype(jnp.float32)
        query_seg = lax.dynamic_slice_in_dim(segment_ids.astype(jnp.int32), offset, rows_per_block, 0)
        key_seg = lax.dynamic_slice_in_dim(padded_seg, offset, rows_per_block + ATTENTION_SPAN, 0)
        query_pos = offset + jnp.arange(rows_per_block, dtype=jnp.int32)
        key_pos = offset - ATTENTION_SPAN + jnp.arange(rows_per_block + ATTENTION_SPAN, dtype=jnp.int32)
        allowed = (query_seg[:, None] == key_seg[None, :]) & (key_pos[None, :] <= query_pos[:, None]) & (key_pos[None, :] > query_pos[:, None] - ATTENTION_SPAN)
        scores = jnp.einsum('qhgd,khd->hgqk', heads_for_queries, heads_for_keys) * score_scale
        scores = jnp.where(allowed[None, None, :, :], scores, masked_score)
        row_max = lax.optimization_barrier(jnp.max(scores, axis=-1, keepdims=True))
        raised = jnp.exp(scores - row_max)
        weights = (raised / lax.optimization_barrier(jnp.sum(raised, axis=-1, keepdims=True))).astype(jnp.bfloat16)
        context = jnp.einsum('hgqk,khd->qhgd', weights.astype(jnp.float32), heads_for_values)
        context_rows = context.reshape(rows_per_block, QUERY_HEADS * HEAD_SIZE).astype(jnp.bfloat16)
        projected = jnp.dot(context_rows, out_proj, preferred_element_type=jnp.float32)
        hidden = lax.dynamic_slice_in_dim(residual, offset, rows_per_block, 0).astype(jnp.float32) + projected
        picked = hidden.reshape(rows_per_block // stride, stride, D)[:, stride - 1, :]
        mean_square = lax.optimization_barrier(jnp.mean(picked * picked, axis=1, keepdims=True))
        normed = (picked * lax.rsqrt(mean_square + 1e-06) * norm_gain.astype(jnp.float32)[None, :]).astype(jnp.bfloat16)
        return (hidden.astype(jnp.bfloat16), normed)
    layer_blocks, normed_blocks = lax.map(attend, jnp.arange(block_count, dtype=jnp.int32))
    layer_out = layer_blocks.reshape(SEQUENCE_TOKENS, D)
    normed_all = normed_blocks.reshape(SCORED, D)
    score_block = 128 if SCORED % 128 == 0 else SCORED
    vocab_ids = jnp.arange(VOCAB, dtype=jnp.int32)

    def score_rows(block_index):
        offset = (block_index * score_block).astype(jnp.int32)
        rows = lax.dynamic_slice_in_dim(normed_all, offset, score_block, 0)
        logits = jnp.dot(rows, head_weight.T, preferred_element_type=jnp.float32)
        row_max = lax.optimization_barrier(jnp.max(logits, axis=1, keepdims=True))
        log_total = row_max + jnp.log(lax.optimization_barrier(jnp.sum(jnp.exp(logits - row_max), axis=1, keepdims=True)))
        log_rows = logits - log_total
        wanted = lax.dynamic_slice_in_dim(next_ids.astype(jnp.int32), offset, score_block, 0)
        target = lax.optimization_barrier(jnp.sum(jnp.where(wanted[:, None] == vocab_ids[None, :], log_rows, 0.0), axis=1))
        return (log_rows, target)
    log_blocks, target_blocks = lax.map(score_rows, jnp.arange(SCORED // score_block, dtype=jnp.int32))
    return (layer_out, log_blocks.reshape(SCORED, VOCAB), target_blocks.reshape(SCORED))
```

```python
import jax
import jax.numpy as jnp
from jax import lax
from jax.sharding import PartitionSpec as P

QUERY_HEADS = 16
KEY_VALUE_HEADS = 8
HEAD_SIZE = 128
ATTENTION_SPAN = 1024
SCORE_DEV = 4
SEG_LANES = 128


score_scale = 168.0 ** (-0.5)
masked_score = -1e30


def forward_one(value, axis):
    count = lax.axis_size(axis)
    return lax.ppermute(value, axis, [(source, source + 1) for source in range(count - 1)])


def gather_rows(value, axis):
    count = lax.axis_size(axis)
    bits = count.bit_length() - 1
    me = lax.axis_index(axis)
    data = value[None]
    for bit in reversed(range(bits)):
        step = 1 << bit
        received = lax.ppermute(data, axis, [(i, i ^ step) for i in range(count)])
        low = ((me >> bit) & 1) == 0
        data = jnp.where(low, jnp.concatenate([data, received], 0), jnp.concatenate([received, data], 0))
    data = data.reshape((2,) * bits + value.shape)
    data = jnp.transpose(data, tuple(reversed(range(bits))) + tuple(range(bits, bits + value.ndim)))
    return data.reshape((count * value.shape[0],) + value.shape[1:])


def normalize(hidden, norm_gain):
    mean_square = jnp.mean(hidden * hidden, axis=1, keepdims=True)
    return (hidden * lax.rsqrt(mean_square + 1e-06) * norm_gain[None, :]).astype(jnp.bfloat16)


def local(
    queries, joined_keys_values, segment_ids, residual, norm_gain, out_proj, head_weight, next_ids
):
    token_rows = queries.shape[0]
    blocks = ATTENTION_SPAN // token_rows
    queries_per_group = QUERY_HEADS // KEY_VALUE_HEADS
    kv_width = joined_keys_values.shape[1]
    my_index = lax.axis_index("seq")
    first_row = my_index * token_rows

    seg_cols = jnp.broadcast_to(segment_ids.astype(jnp.bfloat16)[:, None], (token_rows, SEG_LANES))
    own = jnp.concatenate([joined_keys_values, seg_cols], 1)
    arrived = []
    current = own
    for _ in range(blocks):
        current = forward_one(current, "seq")
        arrived.append(current)
    rim = jnp.concatenate(arrived[::-1], 0)
    rim_kv = rim[:, :kv_width]
    rim_seg = rim[:, kv_width].astype(jnp.int32)
    key_value_pair = jnp.concatenate([rim_kv, joined_keys_values], 0)
    key_seg = jnp.concatenate([rim_seg, segment_ids], 0)
    count_of_keys = key_value_pair.shape[0]
    query_pos = first_row + jnp.arange(token_rows, dtype=jnp.int32)
    key_pos = first_row - blocks * token_rows + jnp.arange(count_of_keys, dtype=jnp.int32)
    allowed = (segment_ids[:, None] == key_seg[None, :]) & (key_pos[None, :] >= 0)
    allowed = (
        allowed
        & (key_pos[None, :] <= query_pos[:, None])
        & (key_pos[None, :] > query_pos[:, None] - ATTENTION_SPAN)
    )
    heads_for_queries = queries.reshape(token_rows, KEY_VALUE_HEADS, queries_per_group, HEAD_SIZE)
    heads_for_keys = key_value_pair[:, : KEY_VALUE_HEADS * HEAD_SIZE].reshape(
        count_of_keys, KEY_VALUE_HEADS, HEAD_SIZE
    )
    heads_for_values = key_value_pair[:, KEY_VALUE_HEADS * HEAD_SIZE :].reshape(
        count_of_keys, KEY_VALUE_HEADS, HEAD_SIZE
    )
    scores = (
        jnp.einsum(
            "qhgd,khd->hgqk", heads_for_queries, heads_for_keys, preferred_element_type=jnp.float32
        )
        * score_scale
    )
    scores = jnp.where(allowed[None, None, :, :], scores, masked_score)
    row_max = jnp.max(scores, axis=-1, keepdims=True)
    raised = jnp.exp(scores - row_max)
    weights = (raised / jnp.sum(raised, axis=-1, keepdims=True)).astype(jnp.bfloat16)
    context = jnp.einsum(
        "hgqk,khd->qhgd", weights, heads_for_values, preferred_element_type=jnp.float32
    )
    context = context.reshape(token_rows, QUERY_HEADS * HEAD_SIZE).astype(jnp.bfloat16)
    width = residual.shape[1]
    projected = jnp.dot(
        context,
        lax.all_gather(out_proj, "seq", axis=0, tiled=True),
        preferred_element_type=jnp.float32,
    )
    hidden = residual.astype(jnp.float32) + projected
    layer_out = hidden.astype(jnp.bfloat16)
    score_count = SCORE_DEV
    stride = token_rows // score_count
    picked = hidden.reshape(score_count, stride, width)[:, stride - 1, :]
    normed = normalize(picked, norm_gain)
    logits = lax.dot_general(
        gather_rows(normed, "seq"),
        head_weight,
        (((1,), (1,)), ((), ())),
        preferred_element_type=jnp.float32,
    )
    vocab_width = head_weight.shape[0]
    local_ids = next_ids - my_index * vocab_width
    vocab_ids = jnp.arange(vocab_width, dtype=jnp.int32)
    shard_max = jnp.max(logits, axis=1)
    shard_total = jnp.sum(jnp.exp(logits - shard_max[:, None]), axis=1)
    shard_pick = jnp.sum(jnp.where(local_ids[:, None] == vocab_ids[None, :], logits, 0.0), axis=1)
    stats = gather_rows(jnp.stack([shard_max, shard_total, shard_pick], 0), "seq")
    stats = stats.reshape(-1, 3, shard_max.shape[0])
    all_max, all_total, all_pick = stats[:, 0], stats[:, 1], stats[:, 2]
    global_max = jnp.max(all_max, axis=0)
    global_total = jnp.sum(all_total * jnp.exp(all_max - global_max[None, :]), axis=0)
    log_total = global_max + jnp.log(global_total)
    log_probs = logits - log_total[:, None]
    target_all = jnp.sum(all_pick, axis=0) - log_total
    target_logp = lax.dynamic_slice_in_dim(target_all, my_index * score_count, score_count, 0)
    return (layer_out, log_probs, target_logp)


def solution(mesh):
    in_specs = (
        P(("parts", "seq"), None),
        P(("parts", "seq"), None),
        P(("parts", "seq")),
        P(("parts", "seq"), None),
        P(),
        P("seq", None),
        P("seq", None),
        P("parts"),
    )
    out_specs = (P(("parts", "seq"), None), P("parts", "seq"), P(("parts", "seq")))
    return jax.shard_map(local, mesh=mesh, in_specs=in_specs, out_specs=out_specs, check_vma=False)
```

```python
import jax
import jax.numpy as jnp
import numpy as np
from jax import lax
from jax.sharding import Mesh
from jax.sharding import PartitionSpec as P

QUERY_HEADS = 16
KEY_VALUE_HEADS = 8
HEAD_SIZE = 128
ATTENTION_SPAN = 1024
SCORE_DEV = 4
SEG_LANES = 128
LANES = 128
CORES = 2
SEQ = ("chip", "core")


score_scale = 168.0 ** (-0.5)
masked_score = -1e30


def seq_count():
    return lax.axis_size("chip") * lax.axis_size("core")


def seq_index():
    return lax.axis_index("chip") * lax.axis_size("core") + lax.axis_index("core")


def forward_one(value):
    count = seq_count()
    return lax.ppermute(value, SEQ, [(source, source + 1) for source in range(count - 1)])


def swap_cores(value):
    return lax.ppermute(value, "core", [(0, 1), (1, 0)])


def gather_rows(value):
    count = seq_count()
    bits = count.bit_length() - 1
    me = seq_index()
    data = value[None]
    for bit in reversed(range(bits)):
        step = 1 << bit
        received = lax.ppermute(data, SEQ, [(i, i ^ step) for i in range(count)])
        low = ((me >> bit) & 1) == 0
        data = jnp.where(low, jnp.concatenate([data, received], 0), jnp.concatenate([received, data], 0))
    data = data.reshape((2,) * bits + value.shape)
    data = jnp.transpose(data, tuple(reversed(range(bits))) + tuple(range(bits, bits + value.ndim)))
    return data.reshape((count * value.shape[0],) + value.shape[1:])


def in_core_order(mine, theirs, first):
    return jnp.where(first, jnp.concatenate([mine, theirs], 0), jnp.concatenate([theirs, mine], 0))


def normalize(hidden, norm_gain):
    mean_square = jnp.mean(hidden * hidden, axis=1, keepdims=True)
    return (hidden * lax.rsqrt(mean_square + 1e-06) * norm_gain[None, :]).astype(jnp.bfloat16)


def local(
    queries, joined_keys_values, segment_ids, residual, norm_gain, out_proj, head_weight, next_ids
):
    token_rows = queries.shape[0]
    blocks = ATTENTION_SPAN // token_rows
    queries_per_group = QUERY_HEADS // KEY_VALUE_HEADS
    kv_width = joined_keys_values.shape[1]
    width = residual.shape[1]
    my_index = seq_index()
    core = lax.axis_index("core")
    first_core = core == 0
    first_row = my_index * token_rows

    half = -(-width // (CORES * LANES)) * LANES
    padded_proj = jnp.pad(out_proj, ((0, 0), (0, CORES * half - width)))
    my_half = lax.dynamic_slice_in_dim(padded_proj, core * half, half, 1)
    other_half = lax.dynamic_slice_in_dim(padded_proj, (1 - core) * half, half, 1)
    chip_proj = in_core_order(my_half, swap_cores(other_half), first_core)
    proj_half = lax.all_gather(chip_proj, "chip", axis=0, tiled=True)

    seg_cols = jnp.broadcast_to(segment_ids.astype(jnp.bfloat16)[:, None], (token_rows, SEG_LANES))
    own = jnp.concatenate([joined_keys_values, seg_cols], 1)
    arrived = []
    current = own
    for _ in range(blocks):
        current = forward_one(current)
        arrived.append(current)
    rim = jnp.concatenate(arrived[::-1], 0)
    rim_kv = rim[:, :kv_width]
    rim_seg = rim[:, kv_width].astype(jnp.int32)
    key_value_pair = jnp.concatenate([rim_kv, joined_keys_values], 0)
    key_seg = jnp.concatenate([rim_seg, segment_ids], 0)
    count_of_keys = key_value_pair.shape[0]
    query_pos = first_row + jnp.arange(token_rows, dtype=jnp.int32)
    key_pos = first_row - blocks * token_rows + jnp.arange(count_of_keys, dtype=jnp.int32)
    allowed = (segment_ids[:, None] == key_seg[None, :]) & (key_pos[None, :] >= 0)
    allowed = (
        allowed
        & (key_pos[None, :] <= query_pos[:, None])
        & (key_pos[None, :] > query_pos[:, None] - ATTENTION_SPAN)
    )
    heads_for_queries = queries.reshape(token_rows, KEY_VALUE_HEADS, queries_per_group, HEAD_SIZE)
    heads_for_keys = key_value_pair[:, : KEY_VALUE_HEADS * HEAD_SIZE].reshape(
        count_of_keys, KEY_VALUE_HEADS, HEAD_SIZE
    )
    heads_for_values = key_value_pair[:, KEY_VALUE_HEADS * HEAD_SIZE :].reshape(
        count_of_keys, KEY_VALUE_HEADS, HEAD_SIZE
    )
    scores = (
        jnp.einsum(
            "qhgd,khd->hgqk", heads_for_queries, heads_for_keys, preferred_element_type=jnp.float32
        )
        * score_scale
    )
    scores = jnp.where(allowed[None, None, :, :], scores, masked_score)
    row_max = jnp.max(scores, axis=-1, keepdims=True)
    raised = jnp.exp(scores - row_max)
    weights = (raised / jnp.sum(raised, axis=-1, keepdims=True)).astype(jnp.bfloat16)
    context = jnp.einsum(
        "hgqk,khd->qhgd", weights, heads_for_values, preferred_element_type=jnp.float32
    )
    context = context.reshape(token_rows, QUERY_HEADS * HEAD_SIZE).astype(jnp.bfloat16)

    chip_context = in_core_order(context, swap_cores(context), first_core)
    chip_projected = jnp.dot(chip_context, proj_half, preferred_element_type=jnp.float32)
    mine = lax.dynamic_slice_in_dim(chip_projected, core * token_rows, token_rows, 0)
    theirs = lax.dynamic_slice_in_dim(chip_projected, (1 - core) * token_rows, token_rows, 0)
    returned = swap_cores(theirs)
    projected = jnp.where(
        first_core, jnp.concatenate([mine, returned], 1), jnp.concatenate([returned, mine], 1)
    )[:, :width]

    hidden = residual.astype(jnp.float32) + projected
    layer_out = hidden.astype(jnp.bfloat16)
    score_count = SCORE_DEV
    stride = token_rows // score_count
    picked = hidden.reshape(score_count, stride, width)[:, stride - 1, :]
    normed = normalize(picked, norm_gain)
    logits = lax.dot_general(
        gather_rows(normed),
        head_weight,
        (((1,), (1,)), ((), ())),
        preferred_element_type=jnp.float32,
    )
    vocab_width = head_weight.shape[0]
    local_ids = next_ids - my_index * vocab_width
    vocab_ids = jnp.arange(vocab_width, dtype=jnp.int32)
    shard_max = jnp.max(logits, axis=1)
    shard_total = jnp.sum(jnp.exp(logits - shard_max[:, None]), axis=1)
    shard_pick = jnp.sum(jnp.where(local_ids[:, None] == vocab_ids[None, :], logits, 0.0), axis=1)
    stats = gather_rows(jnp.stack([shard_max, shard_total, shard_pick], 0))
    stats = stats.reshape(-1, 3, shard_max.shape[0])
    all_max, all_total, all_pick = stats[:, 0], stats[:, 1], stats[:, 2]
    global_max = jnp.max(all_max, axis=0)
    global_total = jnp.sum(all_total * jnp.exp(all_max - global_max[None, :]), axis=0)
    log_total = global_max + jnp.log(global_total)
    log_probs = logits - log_total[:, None]
    target_all = jnp.sum(all_pick, axis=0) - log_total
    target_logp = lax.dynamic_slice_in_dim(target_all, my_index * score_count, score_count, 0)
    return (layer_out, log_probs, target_logp)


def solution(mesh):
    parts, seq = mesh.shape["parts"], mesh.shape["seq"]
    devices = np.asarray(mesh.devices).reshape(parts, seq // CORES, CORES)
    fine = Mesh(devices, ("parts",) + SEQ)
    rows = ("parts",) + SEQ
    in_specs = (
        P(rows, None),
        P(rows, None),
        P(rows),
        P(rows, None),
        P(),
        P(SEQ, None),
        P(SEQ, None),
        P("parts"),
    )
    out_specs = (P(rows, None), P("parts", SEQ), P(rows))
    return jax.shard_map(local, mesh=fine, in_specs=in_specs, out_specs=out_specs, check_vma=False)
```

```python
import jax
import jax.numpy as jnp
import numpy as np
from jax import lax
from jax.sharding import Mesh
from jax.sharding import PartitionSpec as P

QUERY_HEADS = 16
KEY_VALUE_HEADS = 8
HEAD_SIZE = 128
ATTENTION_SPAN = 1024
SCORE_DEV = 4
SEG_LANES = 128
LANES = 128
CORES = 2
SEQ = ("chip", "core")


score_scale = 168.0 ** (-0.5)
masked_score = -1e30


def seq_count():
    return lax.axis_size("chip") * lax.axis_size("core")


def seq_index():
    return lax.axis_index("chip") * lax.axis_size("core") + lax.axis_index("core")


def forward_one(value):
    count = seq_count()
    return lax.ppermute(value, SEQ, [(source, source + 1) for source in range(count - 1)])


def swap_cores(value):
    return lax.ppermute(value, "core", [(0, 1), (1, 0)])


def gather_rows(value):
    count = seq_count()
    bits = count.bit_length() - 1
    me = seq_index()
    data = value[None]
    for bit in reversed(range(bits)):
        step = 1 << bit
        received = lax.ppermute(data, SEQ, [(i, i ^ step) for i in range(count)])
        low = ((me >> bit) & 1) == 0
        data = jnp.where(low, jnp.concatenate([data, received], 0), jnp.concatenate([received, data], 0))
    data = data.reshape((2,) * bits + value.shape)
    data = jnp.transpose(data, tuple(reversed(range(bits))) + tuple(range(bits, bits + value.ndim)))
    return data.reshape((count * value.shape[0],) + value.shape[1:])


def in_core_order(mine, theirs, first):
    return jnp.where(first, jnp.concatenate([mine, theirs], 0), jnp.concatenate([theirs, mine], 0))


def shift_chips(value, chips):
    count = seq_count()
    step = chips * CORES
    return lax.ppermute(value, SEQ, [(s, s + step) for s in range(count - step)])


def across_pair(value, from_odd):
    count = seq_count()
    pairs = [(s, s ^ CORES) for s in range(count) if ((s // CORES) % 2 == 1) == from_odd]
    return lax.ppermute(value, SEQ, pairs)


def halo_window(own, kv_width, blocks, first_core):
    assert blocks == 4 * CORES
    odd = (lax.axis_index("chip") % 2) == 1
    back2 = shift_chips(own, 2)
    own_to_odd = across_pair(own, False)
    partner_own = swap_cores(own)
    back4 = shift_chips(back2, 2)
    back2_to_even = across_pair(back2, True)
    back2_to_odd = across_pair(back2, False)
    back4_to_even = across_pair(back4, True)
    back1 = jnp.where(odd, own_to_odd, back2_to_even)
    back3 = jnp.where(odd, back2_to_odd, back4_to_even)
    near = swap_cores(jnp.stack([back1, back2], 0))
    far = swap_cores(jnp.stack([back3, back4], 0))
    pieces = []
    for mine, theirs in ((back4, far[1]), (back3, far[0]), (back2, near[1]), (back1, near[0]), (own, partner_own)):
        pieces.append(in_core_order(mine, theirs, first_core))
    sequence = jnp.concatenate(pieces, 0)
    token_rows = own.shape[0]
    core = lax.axis_index("core")
    window = lax.dynamic_slice_in_dim(sequence, core * token_rows, (blocks + 1) * token_rows, 0)
    return window[:, :kv_width], window[:, kv_width].astype(jnp.int32)


def normalize(hidden, norm_gain):
    mean_square = jnp.mean(hidden * hidden, axis=1, keepdims=True)
    return (hidden * lax.rsqrt(mean_square + 1e-06) * norm_gain[None, :]).astype(jnp.bfloat16)


def local(
    queries, joined_keys_values, segment_ids, residual, norm_gain, out_proj, head_weight, next_ids
):
    token_rows = queries.shape[0]
    blocks = ATTENTION_SPAN // token_rows
    queries_per_group = QUERY_HEADS // KEY_VALUE_HEADS
    kv_width = joined_keys_values.shape[1]
    width = residual.shape[1]
    my_index = seq_index()
    core = lax.axis_index("core")
    first_core = core == 0
    first_row = my_index * token_rows

    half = -(-width // (CORES * LANES)) * LANES
    padded_proj = jnp.pad(out_proj, ((0, 0), (0, CORES * half - width)))
    my_half = lax.dynamic_slice_in_dim(padded_proj, core * half, half, 1)
    other_half = lax.dynamic_slice_in_dim(padded_proj, (1 - core) * half, half, 1)
    chip_proj = in_core_order(my_half, swap_cores(other_half), first_core)
    proj_half = lax.all_gather(chip_proj, "chip", axis=0, tiled=True)

    seg_cols = jnp.broadcast_to(segment_ids.astype(jnp.bfloat16)[:, None], (token_rows, SEG_LANES))
    own = jnp.concatenate([joined_keys_values, seg_cols], 1)
    key_value_pair, key_seg = halo_window(own, kv_width, blocks, first_core)
    count_of_keys = key_value_pair.shape[0]
    query_pos = first_row + jnp.arange(token_rows, dtype=jnp.int32)
    key_pos = first_row - blocks * token_rows + jnp.arange(count_of_keys, dtype=jnp.int32)
    allowed = (segment_ids[:, None] == key_seg[None, :]) & (key_pos[None, :] >= 0)
    allowed = (
        allowed
        & (key_pos[None, :] <= query_pos[:, None])
        & (key_pos[None, :] > query_pos[:, None] - ATTENTION_SPAN)
    )
    heads_for_queries = queries.reshape(token_rows, KEY_VALUE_HEADS, queries_per_group, HEAD_SIZE)
    heads_for_keys = key_value_pair[:, : KEY_VALUE_HEADS * HEAD_SIZE].reshape(
        count_of_keys, KEY_VALUE_HEADS, HEAD_SIZE
    )
    heads_for_values = key_value_pair[:, KEY_VALUE_HEADS * HEAD_SIZE :].reshape(
        count_of_keys, KEY_VALUE_HEADS, HEAD_SIZE
    )
    scores = (
        jnp.einsum(
            "qhgd,khd->hgqk", heads_for_queries, heads_for_keys, preferred_element_type=jnp.float32
        )
        * score_scale
    )
    scores = jnp.where(allowed[None, None, :, :], scores, masked_score)
    row_max = jnp.max(scores, axis=-1, keepdims=True)
    raised = jnp.exp(scores - row_max)
    weights = (raised / jnp.sum(raised, axis=-1, keepdims=True)).astype(jnp.bfloat16)
    context = jnp.einsum(
        "hgqk,khd->qhgd", weights, heads_for_values, preferred_element_type=jnp.float32
    )
    context = context.reshape(token_rows, QUERY_HEADS * HEAD_SIZE).astype(jnp.bfloat16)

    chip_context = in_core_order(context, swap_cores(context), first_core)
    chip_projected = jnp.dot(chip_context, proj_half, preferred_element_type=jnp.float32)
    mine = lax.dynamic_slice_in_dim(chip_projected, core * token_rows, token_rows, 0)
    theirs = lax.dynamic_slice_in_dim(chip_projected, (1 - core) * token_rows, token_rows, 0)
    returned = swap_cores(theirs)
    projected = jnp.where(
        first_core, jnp.concatenate([mine, returned], 1), jnp.concatenate([returned, mine], 1)
    )[:, :width]

    hidden = residual.astype(jnp.float32) + projected
    layer_out = hidden.astype(jnp.bfloat16)
    score_count = SCORE_DEV
    stride = token_rows // score_count
    picked = hidden.reshape(score_count, stride, width)[:, stride - 1, :]
    normed = normalize(picked, norm_gain)
    logits = lax.dot_general(
        gather_rows(normed),
        head_weight,
        (((1,), (1,)), ((), ())),
        preferred_element_type=jnp.float32,
    )
    vocab_width = head_weight.shape[0]
    local_ids = next_ids - my_index * vocab_width
    vocab_ids = jnp.arange(vocab_width, dtype=jnp.int32)
    shard_max = jnp.max(logits, axis=1)
    shard_total = jnp.sum(jnp.exp(logits - shard_max[:, None]), axis=1)
    shard_pick = jnp.sum(jnp.where(local_ids[:, None] == vocab_ids[None, :], logits, 0.0), axis=1)
    stats = gather_rows(jnp.stack([shard_max, shard_total, shard_pick], 0))
    stats = stats.reshape(-1, 3, shard_max.shape[0])
    all_max, all_total, all_pick = stats[:, 0], stats[:, 1], stats[:, 2]
    global_max = jnp.max(all_max, axis=0)
    global_total = jnp.sum(all_total * jnp.exp(all_max - global_max[None, :]), axis=0)
    log_total = global_max + jnp.log(global_total)
    log_probs = logits - log_total[:, None]
    target_all = jnp.sum(all_pick, axis=0) - log_total
    target_logp = lax.dynamic_slice_in_dim(target_all, my_index * score_count, score_count, 0)
    return (layer_out, log_probs, target_logp)


def solution(mesh):
    parts, seq = mesh.shape["parts"], mesh.shape["seq"]
    devices = np.asarray(mesh.devices).reshape(parts, seq // CORES, CORES)
    fine = Mesh(devices, ("parts",) + SEQ)
    rows = ("parts",) + SEQ
    in_specs = (
        P(rows, None),
        P(rows, None),
        P(rows),
        P(rows, None),
        P(),
        P(SEQ, None),
        P(SEQ, None),
        P("parts"),
    )
    out_specs = (P(rows, None), P("parts", SEQ), P(rows))
    return jax.shard_map(local, mesh=fine, in_specs=in_specs, out_specs=out_specs, check_vma=False)
```

```python
import jax
import jax.numpy as jnp
import numpy as np
from jax import lax
from jax.sharding import Mesh
from jax.sharding import PartitionSpec as P

QUERY_HEADS = 16
KEY_VALUE_HEADS = 8
HEAD_SIZE = 128
ATTENTION_SPAN = 1024
SCORE_DEV = 4
SEG_LANES = 128
LANES = 128
CORES = 2
SEQ = ("chip", "core")


score_scale = 168.0 ** (-0.5)
masked_score = -1e30


def seq_count():
    return lax.axis_size("chip") * lax.axis_size("core")


def seq_index():
    return lax.axis_index("chip") * lax.axis_size("core") + lax.axis_index("core")


def forward_one(value):
    count = seq_count()
    return lax.ppermute(value, SEQ, [(source, source + 1) for source in range(count - 1)])


def swap_cores(value):
    return lax.ppermute(value, "core", [(0, 1), (1, 0)])


def gather_rows(value):
    count = seq_count()
    bits = count.bit_length() - 1
    me = seq_index()
    data = value[None]
    for bit in reversed(range(bits)):
        step = 1 << bit
        received = lax.ppermute(data, SEQ, [(i, i ^ step) for i in range(count)])
        low = ((me >> bit) & 1) == 0
        data = jnp.where(low, jnp.concatenate([data, received], 0), jnp.concatenate([received, data], 0))
    data = data.reshape((2,) * bits + value.shape)
    data = jnp.transpose(data, tuple(reversed(range(bits))) + tuple(range(bits, bits + value.ndim)))
    return data.reshape((count * value.shape[0],) + value.shape[1:])


def in_core_order(mine, theirs, first):
    return jnp.where(first, jnp.concatenate([mine, theirs], 0), jnp.concatenate([theirs, mine], 0))


def shift_chips(value, chips):
    count = seq_count()
    step = chips * CORES
    return lax.ppermute(value, SEQ, [(s, s + step) for s in range(count - step)])


def across_pair(value, from_odd):
    count = seq_count()
    pairs = [(s, s ^ CORES) for s in range(count) if ((s // CORES) % 2 == 1) == from_odd]
    return lax.ppermute(value, SEQ, pairs)


def halo_window(own, kv_width, blocks, first_core):
    assert blocks == 4 * CORES
    odd = (lax.axis_index("chip") % 2) == 1
    back2 = shift_chips(own, 2)
    own_to_odd = across_pair(own, False)
    partner_own = swap_cores(own)
    back4 = shift_chips(back2, 2)
    back2_to_even = across_pair(back2, True)
    back2_to_odd = across_pair(back2, False)
    back4_to_even = across_pair(back4, True)
    back1 = jnp.where(odd, own_to_odd, back2_to_even)
    back3 = jnp.where(odd, back2_to_odd, back4_to_even)
    near = swap_cores(jnp.stack([back1, back2], 0))
    far = swap_cores(jnp.stack([back3, back4], 0))
    pieces = []
    for mine, theirs in ((back4, far[1]), (back3, far[0]), (back2, near[1]), (back1, near[0]), (own, partner_own)):
        pieces.append(in_core_order(mine, theirs, first_core))
    sequence = jnp.concatenate(pieces, 0)
    token_rows = own.shape[0]
    core = lax.axis_index("core")
    window = lax.dynamic_slice_in_dim(sequence, core * token_rows, (blocks + 1) * token_rows, 0)
    return window[:, :kv_width], window[:, kv_width].astype(jnp.int32)


def spread_over_chips(piece):
    chips = lax.axis_size("chip")
    count = seq_count()
    pieces = [piece]
    for d in range(1, chips):
        pieces.append(lax.ppermute(piece, SEQ, [(s, (s + CORES * d) % count) for s in range(count)]))
    return jnp.stack(pieces, 0)


def normalize(hidden, norm_gain):
    mean_square = jnp.mean(hidden * hidden, axis=1, keepdims=True)
    return (hidden * lax.rsqrt(mean_square + 1e-06) * norm_gain[None, :]).astype(jnp.bfloat16)


def local(
    queries, joined_keys_values, segment_ids, residual, norm_gain, out_proj, head_weight, next_ids
):
    token_rows = queries.shape[0]
    blocks = ATTENTION_SPAN // token_rows
    queries_per_group = QUERY_HEADS // KEY_VALUE_HEADS
    kv_width = joined_keys_values.shape[1]
    width = residual.shape[1]
    my_index = seq_index()
    core = lax.axis_index("core")
    first_core = core == 0
    first_row = my_index * token_rows

    half = -(-width // (CORES * LANES)) * LANES
    padded_proj = jnp.pad(out_proj, ((0, 0), (0, CORES * half - width)))
    my_half = lax.dynamic_slice_in_dim(padded_proj, core * half, half, 1)
    other_half = lax.dynamic_slice_in_dim(padded_proj, (1 - core) * half, half, 1)
    chip_proj = in_core_order(my_half, swap_cores(other_half), first_core)
    proj_pieces = spread_over_chips(chip_proj)

    seg_cols = jnp.broadcast_to(segment_ids.astype(jnp.bfloat16)[:, None], (token_rows, SEG_LANES))
    own = jnp.concatenate([joined_keys_values, seg_cols], 1)
    key_value_pair, key_seg = halo_window(own, kv_width, blocks, first_core)
    count_of_keys = key_value_pair.shape[0]
    query_pos = first_row + jnp.arange(token_rows, dtype=jnp.int32)
    key_pos = first_row - blocks * token_rows + jnp.arange(count_of_keys, dtype=jnp.int32)
    allowed = (segment_ids[:, None] == key_seg[None, :]) & (key_pos[None, :] >= 0)
    allowed = (
        allowed
        & (key_pos[None, :] <= query_pos[:, None])
        & (key_pos[None, :] > query_pos[:, None] - ATTENTION_SPAN)
    )
    heads_for_queries = queries.reshape(token_rows, KEY_VALUE_HEADS, queries_per_group, HEAD_SIZE)
    heads_for_keys = key_value_pair[:, : KEY_VALUE_HEADS * HEAD_SIZE].reshape(
        count_of_keys, KEY_VALUE_HEADS, HEAD_SIZE
    )
    heads_for_values = key_value_pair[:, KEY_VALUE_HEADS * HEAD_SIZE :].reshape(
        count_of_keys, KEY_VALUE_HEADS, HEAD_SIZE
    )
    scores = (
        jnp.einsum(
            "qhgd,khd->hgqk", heads_for_queries, heads_for_keys, preferred_element_type=jnp.float32
        )
        * score_scale
    )
    scores = jnp.where(allowed[None, None, :, :], scores, masked_score)
    row_max = jnp.max(scores, axis=-1, keepdims=True)
    raised = jnp.exp(scores - row_max)
    weights = (raised / jnp.sum(raised, axis=-1, keepdims=True)).astype(jnp.bfloat16)
    context = jnp.einsum(
        "hgqk,khd->qhgd", weights, heads_for_values, preferred_element_type=jnp.float32
    )
    context = context.reshape(token_rows, QUERY_HEADS * HEAD_SIZE).astype(jnp.bfloat16)

    chip_context = in_core_order(context, swap_cores(context), first_core)
    chips = lax.axis_size("chip")
    chip_cols = proj_pieces.shape[1]
    chip = lax.axis_index("chip")
    permuted_context = jnp.concatenate(
        [
            lax.dynamic_slice_in_dim(chip_context, ((chip - d) % chips) * chip_cols, chip_cols, 1)
            for d in range(chips)
        ],
        1,
    )
    chip_projected = jnp.dot(
        permuted_context,
        proj_pieces.reshape(chips * proj_pieces.shape[1], proj_pieces.shape[2]),
        preferred_element_type=jnp.float32,
    )
    mine = lax.dynamic_slice_in_dim(chip_projected, core * token_rows, token_rows, 0)
    theirs = lax.dynamic_slice_in_dim(chip_projected, (1 - core) * token_rows, token_rows, 0)
    returned = swap_cores(theirs)
    projected = jnp.where(
        first_core, jnp.concatenate([mine, returned], 1), jnp.concatenate([returned, mine], 1)
    )[:, :width]

    hidden = residual.astype(jnp.float32) + projected
    layer_out = hidden.astype(jnp.bfloat16)
    score_count = SCORE_DEV
    stride = token_rows // score_count
    picked = hidden.reshape(score_count, stride, width)[:, stride - 1, :]
    normed = normalize(picked, norm_gain)
    logits = lax.dot_general(
        gather_rows(normed),
        head_weight,
        (((1,), (1,)), ((), ())),
        preferred_element_type=jnp.float32,
    )
    vocab_width = head_weight.shape[0]
    local_ids = next_ids - my_index * vocab_width
    vocab_ids = jnp.arange(vocab_width, dtype=jnp.int32)
    shard_max = jnp.max(logits, axis=1)
    shard_total = jnp.sum(jnp.exp(logits - shard_max[:, None]), axis=1)
    shard_pick = jnp.sum(jnp.where(local_ids[:, None] == vocab_ids[None, :], logits, 0.0), axis=1)
    stats = gather_rows(jnp.stack([shard_max, shard_total, shard_pick], 0))
    stats = stats.reshape(-1, 3, shard_max.shape[0])
    all_max, all_total, all_pick = stats[:, 0], stats[:, 1], stats[:, 2]
    global_max = jnp.max(all_max, axis=0)
    global_total = jnp.sum(all_total * jnp.exp(all_max - global_max[None, :]), axis=0)
    log_total = global_max + jnp.log(global_total)
    log_probs = logits - log_total[:, None]
    target_all = jnp.sum(all_pick, axis=0) - log_total
    target_logp = lax.dynamic_slice_in_dim(target_all, my_index * score_count, score_count, 0)
    return (layer_out, log_probs, target_logp)


def solution(mesh):
    parts, seq = mesh.shape["parts"], mesh.shape["seq"]
    devices = np.asarray(mesh.devices).reshape(parts, seq // CORES, CORES)
    fine = Mesh(devices, ("parts",) + SEQ)
    rows = ("parts",) + SEQ
    in_specs = (
        P(rows, None),
        P(rows, None),
        P(rows),
        P(rows, None),
        P(),
        P(SEQ, None),
        P(SEQ, None),
        P("parts"),
    )
    out_specs = (P(rows, None), P("parts", SEQ), P(rows))
    return jax.shard_map(local, mesh=fine, in_specs=in_specs, out_specs=out_specs, check_vma=False)
```

```python
import jax
import jax.numpy as jnp
import numpy as np
from jax import lax
from jax.sharding import Mesh
from jax.sharding import PartitionSpec as P

QUERY_HEADS = 16
KEY_VALUE_HEADS = 8
HEAD_SIZE = 128
ATTENTION_SPAN = 1024
SCORE_DEV = 4
SEG_LANES = 128
LANES = 128
CORES = 2
SEQ = ("chip", "core")


score_scale = 168.0 ** (-0.5)
masked_score = -1e30


def seq_count():
    return lax.axis_size("chip") * lax.axis_size("core")


def seq_index():
    return lax.axis_index("chip") * lax.axis_size("core") + lax.axis_index("core")


def forward_one(value):
    count = seq_count()
    return lax.ppermute(value, SEQ, [(source, source + 1) for source in range(count - 1)])


def swap_cores(value):
    return lax.ppermute(value, "core", [(0, 1), (1, 0)])


def gather_rows(value):
    count = seq_count()
    bits = count.bit_length() - 1
    me = seq_index()
    data = value[None]
    for bit in reversed(range(bits)):
        step = 1 << bit
        received = lax.ppermute(data, SEQ, [(i, i ^ step) for i in range(count)])
        low = ((me >> bit) & 1) == 0
        data = jnp.where(low, jnp.concatenate([data, received], 0), jnp.concatenate([received, data], 0))
    data = data.reshape((2,) * bits + value.shape)
    data = jnp.transpose(data, tuple(reversed(range(bits))) + tuple(range(bits, bits + value.ndim)))
    return data.reshape((count * value.shape[0],) + value.shape[1:])


def in_core_order(mine, theirs, first):
    return jnp.where(first, jnp.concatenate([mine, theirs], 0), jnp.concatenate([theirs, mine], 0))


def shift_chips(value, chips):
    count = seq_count()
    step = chips * CORES
    return lax.ppermute(value, SEQ, [(s, s + step) for s in range(count - step)])


def across_pair(value, from_odd):
    count = seq_count()
    pairs = [(s, s ^ CORES) for s in range(count) if ((s // CORES) % 2 == 1) == from_odd]
    return lax.ppermute(value, SEQ, pairs)


def halo_window(own, kv_width, blocks, first_core):
    assert blocks == 4 * CORES
    odd = (lax.axis_index("chip") % 2) == 1
    back2 = shift_chips(own, 2)
    own_to_odd = across_pair(own, False)
    partner_own = swap_cores(own)
    back4 = shift_chips(back2, 2)
    back2_to_even = across_pair(back2, True)
    back2_to_odd = across_pair(back2, False)
    back4_to_even = across_pair(back4, True)
    back1 = jnp.where(odd, own_to_odd, back2_to_even)
    back3 = jnp.where(odd, back2_to_odd, back4_to_even)
    near = swap_cores(jnp.stack([back1, back2], 0))
    far = swap_cores(jnp.stack([back3, back4], 0))
    pieces = []
    for mine, theirs in ((back4, far[1]), (back3, far[0]), (back2, near[1]), (back1, near[0]), (own, partner_own)):
        pieces.append(in_core_order(mine, theirs, first_core))
    sequence = jnp.concatenate(pieces, 0)
    token_rows = own.shape[0]
    core = lax.axis_index("core")
    window = lax.dynamic_slice_in_dim(sequence, core * token_rows, (blocks + 1) * token_rows, 0)
    return window[:, :kv_width], window[:, kv_width].astype(jnp.int32)


def normalize(hidden, norm_gain):
    mean_square = jnp.mean(hidden * hidden, axis=1, keepdims=True)
    return (hidden * lax.rsqrt(mean_square + 1e-06) * norm_gain[None, :]).astype(jnp.bfloat16)


def local(
    queries, joined_keys_values, segment_ids, residual, norm_gain, out_proj, head_weight, next_ids
):
    token_rows = queries.shape[0]
    blocks = ATTENTION_SPAN // token_rows
    queries_per_group = QUERY_HEADS // KEY_VALUE_HEADS
    kv_width = joined_keys_values.shape[1]
    width = residual.shape[1]
    my_index = seq_index()
    core = lax.axis_index("core")
    first_core = core == 0
    first_row = my_index * token_rows

    full_proj = lax.all_gather(out_proj, SEQ, axis=0, tiled=True)

    seg_cols = jnp.broadcast_to(segment_ids.astype(jnp.bfloat16)[:, None], (token_rows, SEG_LANES))
    own = jnp.concatenate([joined_keys_values, seg_cols], 1)
    key_value_pair, key_seg = halo_window(own, kv_width, blocks, first_core)
    count_of_keys = key_value_pair.shape[0]
    query_pos = first_row + jnp.arange(token_rows, dtype=jnp.int32)
    key_pos = first_row - blocks * token_rows + jnp.arange(count_of_keys, dtype=jnp.int32)
    allowed = (segment_ids[:, None] == key_seg[None, :]) & (key_pos[None, :] >= 0)
    allowed = (
        allowed
        & (key_pos[None, :] <= query_pos[:, None])
        & (key_pos[None, :] > query_pos[:, None] - ATTENTION_SPAN)
    )
    heads_for_queries = queries.reshape(token_rows, KEY_VALUE_HEADS, queries_per_group, HEAD_SIZE)
    heads_for_keys = key_value_pair[:, : KEY_VALUE_HEADS * HEAD_SIZE].reshape(
        count_of_keys, KEY_VALUE_HEADS, HEAD_SIZE
    )
    heads_for_values = key_value_pair[:, KEY_VALUE_HEADS * HEAD_SIZE :].reshape(
        count_of_keys, KEY_VALUE_HEADS, HEAD_SIZE
    )
    scores = (
        jnp.einsum(
            "qhgd,khd->hgqk", heads_for_queries, heads_for_keys, preferred_element_type=jnp.float32
        )
        * score_scale
    )
    scores = jnp.where(allowed[None, None, :, :], scores, masked_score)
    row_max = jnp.max(scores, axis=-1, keepdims=True)
    raised = jnp.exp(scores - row_max)
    weights = (raised / jnp.sum(raised, axis=-1, keepdims=True)).astype(jnp.bfloat16)
    context = jnp.einsum(
        "hgqk,khd->qhgd", weights, heads_for_values, preferred_element_type=jnp.float32
    )
    context = context.reshape(token_rows, QUERY_HEADS * HEAD_SIZE).astype(jnp.bfloat16)

    score_count = SCORE_DEV
    stride = token_rows // score_count
    scored_context = context.reshape(score_count, stride, -1)[:, stride - 1, :]
    scored_residual = residual.reshape(score_count, stride, width)[:, stride - 1, :]
    picked = scored_residual.astype(jnp.float32) + jnp.dot(
        scored_context, full_proj, preferred_element_type=jnp.float32
    )
    normed = normalize(picked, norm_gain)
    projected = jnp.dot(context, full_proj, preferred_element_type=jnp.float32)
    hidden = residual.astype(jnp.float32) + projected
    layer_out = hidden.astype(jnp.bfloat16)
    logits = lax.dot_general(
        gather_rows(normed),
        head_weight,
        (((1,), (1,)), ((), ())),
        preferred_element_type=jnp.float32,
    )
    vocab_width = head_weight.shape[0]
    local_ids = next_ids - my_index * vocab_width
    vocab_ids = jnp.arange(vocab_width, dtype=jnp.int32)
    shard_max = jnp.max(logits, axis=1)
    shard_total = jnp.sum(jnp.exp(logits - shard_max[:, None]), axis=1)
    shard_pick = jnp.sum(jnp.where(local_ids[:, None] == vocab_ids[None, :], logits, 0.0), axis=1)
    stats = gather_rows(jnp.stack([shard_max, shard_total, shard_pick], 0))
    stats = stats.reshape(-1, 3, shard_max.shape[0])
    all_max, all_total, all_pick = stats[:, 0], stats[:, 1], stats[:, 2]
    global_max = jnp.max(all_max, axis=0)
    global_total = jnp.sum(all_total * jnp.exp(all_max - global_max[None, :]), axis=0)
    log_total = global_max + jnp.log(global_total)
    log_probs = logits - log_total[:, None]
    target_all = jnp.sum(all_pick, axis=0) - log_total
    target_logp = lax.dynamic_slice_in_dim(target_all, my_index * score_count, score_count, 0)
    return (layer_out, log_probs, target_logp)


def solution(mesh):
    parts, seq = mesh.shape["parts"], mesh.shape["seq"]
    devices = np.asarray(mesh.devices).reshape(parts, seq // CORES, CORES)
    fine = Mesh(devices, ("parts",) + SEQ)
    rows = ("parts",) + SEQ
    in_specs = (
        P(rows, None),
        P(rows, None),
        P(rows),
        P(rows, None),
        P(),
        P(SEQ, None),
        P(SEQ, None),
        P("parts"),
    )
    out_specs = (P(rows, None), P("parts", SEQ), P(rows))
    return jax.shard_map(local, mesh=fine, in_specs=in_specs, out_specs=out_specs, check_vma=False)
```

```python
import jax
import jax.numpy as jnp
import numpy as np
from jax import lax
from jax.sharding import Mesh
from jax.sharding import PartitionSpec as P

QUERY_HEADS = 16
KEY_VALUE_HEADS = 8
HEAD_SIZE = 128
ATTENTION_SPAN = 1024
SCORE_DEV = 4
SEG_LANES = 128
LANES = 128
CORES = 2
SEQ = ("chip", "core")


score_scale = 168.0 ** (-0.5)
masked_score = -1e30


def seq_count():
    return lax.axis_size("chip") * lax.axis_size("core")


def seq_index():
    return lax.axis_index("chip") * lax.axis_size("core") + lax.axis_index("core")


def forward_one(value):
    count = seq_count()
    return lax.ppermute(value, SEQ, [(source, source + 1) for source in range(count - 1)])


def swap_cores(value):
    return lax.ppermute(value, "core", [(0, 1), (1, 0)])


def gather_rows(value, radix=4):
    count = seq_count()
    me = seq_index()
    data = value[None]
    stride = 1
    while stride < count:
        digits = min(radix, count // stride)
        mine = (me // stride) % digits
        received = [data]
        for offset in range(1, digits):
            pairs = []
            for i in range(count):
                d = (i // stride) % digits
                pairs.append((i, i + (((d + offset) % digits) - d) * stride))
            received.append(lax.ppermute(data, SEQ, pairs))
        stacked = jnp.stack(received, 0)
        order = (mine - jnp.arange(digits)) % digits
        data = jnp.take(stacked, order, axis=0)
        data = data.reshape((digits * data.shape[1],) + data.shape[2:])
        stride *= digits
    return data.reshape((count * value.shape[0],) + value.shape[1:])


def in_core_order(mine, theirs, first):
    return jnp.where(first, jnp.concatenate([mine, theirs], 0), jnp.concatenate([theirs, mine], 0))


def shift_chips(value, chips):
    count = seq_count()
    step = chips * CORES
    return lax.ppermute(value, SEQ, [(s, s + step) for s in range(count - step)])


def across_pair(value, from_odd):
    count = seq_count()
    pairs = [(s, s ^ CORES) for s in range(count) if ((s // CORES) % 2 == 1) == from_odd]
    return lax.ppermute(value, SEQ, pairs)


def halo_window(own, kv_width, blocks, first_core):
    assert blocks == 4 * CORES
    odd = (lax.axis_index("chip") % 2) == 1
    back2 = shift_chips(own, 2)
    own_to_odd = across_pair(own, False)
    partner_own = swap_cores(own)
    back4 = shift_chips(back2, 2)
    back2_to_even = across_pair(back2, True)
    back2_to_odd = across_pair(back2, False)
    back4_to_even = across_pair(back4, True)
    back1 = jnp.where(odd, own_to_odd, back2_to_even)
    back3 = jnp.where(odd, back2_to_odd, back4_to_even)
    near = swap_cores(jnp.stack([back1, back2], 0))
    far = swap_cores(jnp.stack([back3, back4], 0))
    pieces = []
    for mine, theirs in ((back4, far[1]), (back3, far[0]), (back2, near[1]), (back1, near[0]), (own, partner_own)):
        pieces.append(in_core_order(mine, theirs, first_core))
    sequence = jnp.concatenate(pieces, 0)
    token_rows = own.shape[0]
    core = lax.axis_index("core")
    window = lax.dynamic_slice_in_dim(sequence, core * token_rows, (blocks + 1) * token_rows, 0)
    return window[:, :kv_width], window[:, kv_width].astype(jnp.int32)


def normalize(hidden, norm_gain):
    mean_square = jnp.mean(hidden * hidden, axis=1, keepdims=True)
    return (hidden * lax.rsqrt(mean_square + 1e-06) * norm_gain[None, :]).astype(jnp.bfloat16)


def local(
    queries, joined_keys_values, segment_ids, residual, norm_gain, out_proj, head_weight, next_ids
):
    token_rows = queries.shape[0]
    blocks = ATTENTION_SPAN // token_rows
    queries_per_group = QUERY_HEADS // KEY_VALUE_HEADS
    kv_width = joined_keys_values.shape[1]
    width = residual.shape[1]
    my_index = seq_index()
    core = lax.axis_index("core")
    first_core = core == 0
    first_row = my_index * token_rows

    full_proj = lax.all_gather(out_proj, SEQ, axis=0, tiled=True)

    seg_cols = jnp.broadcast_to(segment_ids.astype(jnp.bfloat16)[:, None], (token_rows, SEG_LANES))
    own = jnp.concatenate([joined_keys_values, seg_cols], 1)
    key_value_pair, key_seg = halo_window(own, kv_width, blocks, first_core)
    count_of_keys = key_value_pair.shape[0]
    query_pos = first_row + jnp.arange(token_rows, dtype=jnp.int32)
    key_pos = first_row - blocks * token_rows + jnp.arange(count_of_keys, dtype=jnp.int32)
    allowed = (segment_ids[:, None] == key_seg[None, :]) & (key_pos[None, :] >= 0)
    allowed = (
        allowed
        & (key_pos[None, :] <= query_pos[:, None])
        & (key_pos[None, :] > query_pos[:, None] - ATTENTION_SPAN)
    )
    heads_for_queries = queries.reshape(token_rows, KEY_VALUE_HEADS, queries_per_group, HEAD_SIZE)
    heads_for_keys = key_value_pair[:, : KEY_VALUE_HEADS * HEAD_SIZE].reshape(
        count_of_keys, KEY_VALUE_HEADS, HEAD_SIZE
    )
    heads_for_values = key_value_pair[:, KEY_VALUE_HEADS * HEAD_SIZE :].reshape(
        count_of_keys, KEY_VALUE_HEADS, HEAD_SIZE
    )
    scores = (
        jnp.einsum(
            "qhgd,khd->hgqk", heads_for_queries, heads_for_keys, preferred_element_type=jnp.float32
        )
        * score_scale
    )
    scores = jnp.where(allowed[None, None, :, :], scores, masked_score)
    row_max = jnp.max(scores, axis=-1, keepdims=True)
    raised = jnp.exp(scores - row_max)
    weights = (raised / jnp.sum(raised, axis=-1, keepdims=True)).astype(jnp.bfloat16)
    context = jnp.einsum(
        "hgqk,khd->qhgd", weights, heads_for_values, preferred_element_type=jnp.float32
    )
    context = context.reshape(token_rows, QUERY_HEADS * HEAD_SIZE).astype(jnp.bfloat16)

    score_count = SCORE_DEV
    stride = token_rows // score_count
    projected = jnp.dot(context, full_proj, preferred_element_type=jnp.float32)
    hidden = residual.astype(jnp.float32) + projected
    layer_out = hidden.astype(jnp.bfloat16)
    picked = hidden.reshape(score_count, stride, width)[:, stride - 1, :]
    normed = normalize(picked, norm_gain)
    logits = lax.dot_general(
        gather_rows(normed),
        head_weight,
        (((1,), (1,)), ((), ())),
        preferred_element_type=jnp.float32,
    )
    vocab_width = head_weight.shape[0]
    local_ids = next_ids - my_index * vocab_width
    vocab_ids = jnp.arange(vocab_width, dtype=jnp.int32)
    shard_max = jnp.max(logits, axis=1)
    shard_total = jnp.sum(jnp.exp(logits - shard_max[:, None]), axis=1)
    shard_pick = jnp.sum(jnp.where(local_ids[:, None] == vocab_ids[None, :], logits, 0.0), axis=1)
    stats = gather_rows(jnp.stack([shard_max, shard_total, shard_pick], 0))
    stats = stats.reshape(-1, 3, shard_max.shape[0])
    all_max, all_total, all_pick = stats[:, 0], stats[:, 1], stats[:, 2]
    global_max = jnp.max(all_max, axis=0)
    global_total = jnp.sum(all_total * jnp.exp(all_max - global_max[None, :]), axis=0)
    log_total = global_max + jnp.log(global_total)
    log_probs = logits - log_total[:, None]
    target_all = jnp.sum(all_pick, axis=0) - log_total
    target_logp = lax.dynamic_slice_in_dim(target_all, my_index * score_count, score_count, 0)
    return (layer_out, log_probs, target_logp)


def solution(mesh):
    parts, seq = mesh.shape["parts"], mesh.shape["seq"]
    devices = np.asarray(mesh.devices).reshape(parts, seq // CORES, CORES)
    fine = Mesh(devices, ("parts",) + SEQ)
    rows = ("parts",) + SEQ
    in_specs = (
        P(rows, None),
        P(rows, None),
        P(rows),
        P(rows, None),
        P(),
        P(SEQ, None),
        P(SEQ, None),
        P("parts"),
    )
    out_specs = (P(rows, None), P("parts", SEQ), P(rows))
    return jax.shard_map(local, mesh=fine, in_specs=in_specs, out_specs=out_specs, check_vma=False)
```

```python
import jax
import jax.numpy as jnp
import numpy as np
from jax import lax
from jax.sharding import Mesh
from jax.sharding import PartitionSpec as P

QUERY_HEADS = 16
KEY_VALUE_HEADS = 8
HEAD_SIZE = 128
ATTENTION_SPAN = 1024
SCORE_DEV = 4
SEG_LANES = 128
LANES = 128
CORES = 2
SEQ = ("chip", "core")


score_scale = 168.0 ** (-0.5)
masked_score = -1e30


def seq_count():
    return lax.axis_size("chip") * lax.axis_size("core")


def seq_index():
    return lax.axis_index("chip") * lax.axis_size("core") + lax.axis_index("core")


def forward_one(value):
    count = seq_count()
    return lax.ppermute(value, SEQ, [(source, source + 1) for source in range(count - 1)])


def swap_cores(value):
    return lax.ppermute(value, "core", [(0, 1), (1, 0)])


def gather_rows(value, radix=4):
    count = seq_count()
    me = seq_index()
    data = value[None]
    stride = 1
    while stride < count:
        digits = min(radix, count // stride)
        mine = (me // stride) % digits
        received = [data]
        for offset in range(1, digits):
            pairs = []
            for i in range(count):
                d = (i // stride) % digits
                pairs.append((i, i + (((d + offset) % digits) - d) * stride))
            received.append(lax.ppermute(data, SEQ, pairs))
        stacked = jnp.stack(received, 0)
        order = (mine - jnp.arange(digits)) % digits
        data = jnp.take(stacked, order, axis=0)
        data = data.reshape((digits * data.shape[1],) + data.shape[2:])
        stride *= digits
    return data.reshape((count * value.shape[0],) + value.shape[1:])


def in_core_order(mine, theirs, first):
    return jnp.where(first, jnp.concatenate([mine, theirs], 0), jnp.concatenate([theirs, mine], 0))


def shift_chips(value, chips):
    count = seq_count()
    step = chips * CORES
    return lax.ppermute(value, SEQ, [(s, s + step) for s in range(count - step)])


def across_pair(value, from_odd):
    count = seq_count()
    pairs = [(s, s ^ CORES) for s in range(count) if ((s // CORES) % 2 == 1) == from_odd]
    return lax.ppermute(value, SEQ, pairs)


def halo_window(own, kv_width, blocks, first_core):
    assert blocks == 4 * CORES
    odd = (lax.axis_index("chip") % 2) == 1
    back2 = shift_chips(own, 2)
    own_to_odd = across_pair(own, False)
    partner_own = swap_cores(own)
    back4 = shift_chips(back2, 2)
    back2_to_even = across_pair(back2, True)
    back2_to_odd = across_pair(back2, False)
    back4_to_even = across_pair(back4, True)
    back1 = jnp.where(odd, own_to_odd, back2_to_even)
    back3 = jnp.where(odd, back2_to_odd, back4_to_even)
    near = swap_cores(jnp.stack([back1, back2], 0))
    far = swap_cores(jnp.stack([back3, back4], 0))
    pieces = []
    for mine, theirs in ((back4, far[1]), (back3, far[0]), (back2, near[1]), (back1, near[0]), (own, partner_own)):
        pieces.append(in_core_order(mine, theirs, first_core))
    sequence = jnp.concatenate(pieces, 0)
    token_rows = own.shape[0]
    core = lax.axis_index("core")
    window = lax.dynamic_slice_in_dim(sequence, core * token_rows, (blocks + 1) * token_rows, 0)
    return window[:, :kv_width], window[:, kv_width].astype(jnp.int32)


def normalize(hidden, norm_gain):
    mean_square = jnp.mean(hidden * hidden, axis=1, keepdims=True)
    return (hidden * lax.rsqrt(mean_square + 1e-06) * norm_gain[None, :]).astype(jnp.bfloat16)


def local(
    queries, joined_keys_values, segment_ids, residual, norm_gain, out_proj, head_weight, next_ids
):
    token_rows = queries.shape[0]
    blocks = ATTENTION_SPAN // token_rows
    queries_per_group = QUERY_HEADS // KEY_VALUE_HEADS
    kv_width = joined_keys_values.shape[1]
    width = residual.shape[1]
    my_index = seq_index()
    core = lax.axis_index("core")
    first_core = core == 0
    first_row = my_index * token_rows

    full_proj = lax.all_gather(out_proj, SEQ, axis=0, tiled=True)
    score_count = SCORE_DEV
    stride = token_rows // score_count
    scored_residual = gather_rows(residual.reshape(score_count, stride, width)[:, stride - 1, :])

    seg_cols = jnp.broadcast_to(segment_ids.astype(jnp.bfloat16)[:, None], (token_rows, SEG_LANES))
    own = jnp.concatenate([joined_keys_values, seg_cols], 1)
    key_value_pair, key_seg = halo_window(own, kv_width, blocks, first_core)
    count_of_keys = key_value_pair.shape[0]
    query_pos = first_row + jnp.arange(token_rows, dtype=jnp.int32)
    key_pos = first_row - blocks * token_rows + jnp.arange(count_of_keys, dtype=jnp.int32)
    allowed = (segment_ids[:, None] == key_seg[None, :]) & (key_pos[None, :] >= 0)
    allowed = (
        allowed
        & (key_pos[None, :] <= query_pos[:, None])
        & (key_pos[None, :] > query_pos[:, None] - ATTENTION_SPAN)
    )
    heads_for_queries = queries.reshape(token_rows, KEY_VALUE_HEADS, queries_per_group, HEAD_SIZE)
    heads_for_keys = key_value_pair[:, : KEY_VALUE_HEADS * HEAD_SIZE].reshape(
        count_of_keys, KEY_VALUE_HEADS, HEAD_SIZE
    )
    heads_for_values = key_value_pair[:, KEY_VALUE_HEADS * HEAD_SIZE :].reshape(
        count_of_keys, KEY_VALUE_HEADS, HEAD_SIZE
    )
    scores = (
        jnp.einsum(
            "qhgd,khd->hgqk", heads_for_queries, heads_for_keys, preferred_element_type=jnp.float32
        )
        * score_scale
    )
    scores = jnp.where(allowed[None, None, :, :], scores, masked_score)
    row_max = jnp.max(scores, axis=-1, keepdims=True)
    raised = jnp.exp(scores - row_max)
    weights = (raised / jnp.sum(raised, axis=-1, keepdims=True)).astype(jnp.bfloat16)
    context = jnp.einsum(
        "hgqk,khd->qhgd", weights, heads_for_values, preferred_element_type=jnp.float32
    )
    context = context.reshape(token_rows, QUERY_HEADS * HEAD_SIZE).astype(jnp.bfloat16)

    scored_context = gather_rows(context.reshape(score_count, stride, -1)[:, stride - 1, :])
    picked = scored_residual.astype(jnp.float32) + jnp.dot(
        scored_context, full_proj, preferred_element_type=jnp.float32
    )
    normed = normalize(picked, norm_gain)
    projected = jnp.dot(context, full_proj, preferred_element_type=jnp.float32)
    hidden = residual.astype(jnp.float32) + projected
    layer_out = hidden.astype(jnp.bfloat16)
    logits = lax.dot_general(
        normed,
        head_weight,
        (((1,), (1,)), ((), ())),
        preferred_element_type=jnp.float32,
    )
    vocab_width = head_weight.shape[0]
    local_ids = next_ids - my_index * vocab_width
    vocab_ids = jnp.arange(vocab_width, dtype=jnp.int32)
    shard_max = jnp.max(logits, axis=1)
    shard_total = jnp.sum(jnp.exp(logits - shard_max[:, None]), axis=1)
    shard_pick = jnp.sum(jnp.where(local_ids[:, None] == vocab_ids[None, :], logits, 0.0), axis=1)
    stats = gather_rows(jnp.stack([shard_max, shard_total, shard_pick], 0))
    stats = stats.reshape(-1, 3, shard_max.shape[0])
    all_max, all_total, all_pick = stats[:, 0], stats[:, 1], stats[:, 2]
    global_max = jnp.max(all_max, axis=0)
    global_total = jnp.sum(all_total * jnp.exp(all_max - global_max[None, :]), axis=0)
    log_total = global_max + jnp.log(global_total)
    log_probs = logits - log_total[:, None]
    target_all = jnp.sum(all_pick, axis=0) - log_total
    target_logp = lax.dynamic_slice_in_dim(target_all, my_index * score_count, score_count, 0)
    return (layer_out, log_probs, target_logp)


def solution(mesh):
    parts, seq = mesh.shape["parts"], mesh.shape["seq"]
    devices = np.asarray(mesh.devices).reshape(parts, seq // CORES, CORES)
    fine = Mesh(devices, ("parts",) + SEQ)
    rows = ("parts",) + SEQ
    in_specs = (
        P(rows, None),
        P(rows, None),
        P(rows),
        P(rows, None),
        P(),
        P(SEQ, None),
        P(SEQ, None),
        P("parts"),
    )
    out_specs = (P(rows, None), P("parts", SEQ), P(rows))
    return jax.shard_map(local, mesh=fine, in_specs=in_specs, out_specs=out_specs, check_vma=False)
```

```python
import functools

import jax
import jax.numpy as jnp
import numpy as np
from jax import lax
from jax.sharding import Mesh
from jax.sharding import PartitionSpec as P

QUERY_HEADS = 16
KEY_VALUE_HEADS = 8
HEAD_SIZE = 128
ATTENTION_SPAN = 1024
SCORE_DEV = 4
SEG_LANES = 128
LANES = 128
CORES = 2
SEQ = ("chip", "core")
RING_CHIPS = 8


score_scale = 168.0 ** (-0.5)
masked_score = -1e30


def seq_count():
    return lax.axis_size("chip") * lax.axis_size("core")


def seq_index():
    return lax.axis_index("chip") * lax.axis_size("core") + lax.axis_index("core")


def forward_one(value):
    count = seq_count()
    return lax.ppermute(value, SEQ, [(source, source + 1) for source in range(count - 1)])


def swap_cores(value):
    return lax.ppermute(value, "core", [(0, 1), (1, 0)])


def gather_rows(value, radix=4):
    count = seq_count()
    me = seq_index()
    data = value[None]
    stride = 1
    while stride < count:
        digits = min(radix, count // stride)
        mine = (me // stride) % digits
        received = [data]
        for offset in range(1, digits):
            pairs = []
            for i in range(count):
                d = (i // stride) % digits
                pairs.append((i, i + (((d + offset) % digits) - d) * stride))
            received.append(lax.ppermute(data, SEQ, pairs))
        stacked = jnp.stack(received, 0)
        order = (mine - jnp.arange(digits)) % digits
        data = jnp.take(stacked, order, axis=0)
        data = data.reshape((digits * data.shape[1],) + data.shape[2:])
        stride *= digits
    return data.reshape((count * value.shape[0],) + value.shape[1:])


def in_core_order(mine, theirs, first):
    return jnp.where(first, jnp.concatenate([mine, theirs], 0), jnp.concatenate([theirs, mine], 0))


def shift_chips(value, chips):
    count = seq_count()
    step = chips * CORES
    return lax.ppermute(value, SEQ, [(s, s + step) for s in range(count - step)])


def across_pair(value, from_odd):
    count = seq_count()
    pairs = [(s, s ^ CORES) for s in range(count) if ((s // CORES) % 2 == 1) == from_odd]
    return lax.ppermute(value, SEQ, pairs)


def halo_window(own, kv_width, blocks, first_core):
    assert blocks == 4 * CORES
    odd = (lax.axis_index("chip") % 2) == 1
    back2 = shift_chips(own, 2)
    own_to_odd = across_pair(own, False)
    partner_own = swap_cores(own)
    back4 = shift_chips(back2, 2)
    back2_to_even = across_pair(back2, True)
    back2_to_odd = across_pair(back2, False)
    back4_to_even = across_pair(back4, True)
    back1 = jnp.where(odd, own_to_odd, back2_to_even)
    back3 = jnp.where(odd, back2_to_odd, back4_to_even)
    near = swap_cores(jnp.stack([back1, back2], 0))
    far = swap_cores(jnp.stack([back3, back4], 0))
    pieces = []
    for mine, theirs in ((back4, far[1]), (back3, far[0]), (back2, near[1]), (back1, near[0]), (own, partner_own)):
        pieces.append(in_core_order(mine, theirs, first_core))
    sequence = jnp.concatenate(pieces, 0)
    token_rows = own.shape[0]
    core = lax.axis_index("core")
    window = lax.dynamic_slice_in_dim(sequence, core * token_rows, (blocks + 1) * token_rows, 0)
    return window[:, :kv_width], window[:, kv_width].astype(jnp.int32)


def chip_cycle(mesh):
    chips = mesh.shape["seq"] // CORES
    try:
        coords = [tuple(d.coords) for d in np.asarray(mesh.devices)[0, ::CORES]]
        moving = [a for a in range(len(coords[0])) if coords[0][a] != coords[1][a]][0]
        fast = 1
        while fast < chips and coords[fast][moving] != coords[0][moving]:
            fast += 1
    except Exception:
        fast = 2
    slow = chips // fast
    if chips % fast or (slow % 2 and fast % 2) or fast < 2:
        return list(range(chips))
    if slow % 2:
        path = [c for c in range(fast)]
        for c in range(fast - 1, -1, -1):
            rows = range(1, slow) if (fast - 1 - c) % 2 == 0 else range(slow - 1, 0, -1)
            path += [r * fast + c for r in rows]
        return path
    path = [r * fast for r in range(slow)]
    for r in range(slow - 1, -1, -1):
        cols = range(1, fast) if (slow - 1 - r) % 2 == 0 else range(fast - 1, 0, -1)
        path += [r * fast + c for c in cols]
    return path


def ring_gather(piece, cycle):
    chips = len(cycle)
    count = seq_count()
    position = [0] * chips
    for p, k in enumerate(cycle):
        position[k] = p
    ahead = {k: cycle[(position[k] + 1) % chips] for k in range(chips)}
    behind = {k: cycle[(position[k] - 1) % chips] for k in range(chips)}
    forward = [(s, ahead[s // CORES] * CORES + s % CORES) for s in range(count)]
    backward = [(s, behind[s // CORES] * CORES + s % CORES) for s in range(count)]
    me = jnp.asarray(position, jnp.int32)[lax.axis_index("chip")]
    order = jnp.asarray(cycle, jnp.int32)
    slots, sources = [piece], [order[me]]
    current = piece
    for step in range(1, chips // 2 + 1):
        current = lax.ppermute(current, SEQ, forward)
        slots.append(current)
        sources.append(order[(me - step) % chips])
    current = piece
    for step in range(1, (chips - 1) // 2 + 1):
        current = lax.ppermute(current, SEQ, backward)
        slots.append(current)
        sources.append(order[(me + step) % chips])
    return slots, sources


def normalize(hidden, norm_gain):
    mean_square = jnp.mean(hidden * hidden, axis=1, keepdims=True)
    return (hidden * lax.rsqrt(mean_square + 1e-06) * norm_gain[None, :]).astype(jnp.bfloat16)


def local(
    cycle,
    queries, joined_keys_values, segment_ids, residual, norm_gain, out_proj, head_weight, next_ids
):
    token_rows = queries.shape[0]
    blocks = ATTENTION_SPAN // token_rows
    queries_per_group = QUERY_HEADS // KEY_VALUE_HEADS
    kv_width = joined_keys_values.shape[1]
    width = residual.shape[1]
    my_index = seq_index()
    core = lax.axis_index("core")
    first_core = core == 0
    first_row = my_index * token_rows

    if len(cycle) <= RING_CHIPS:
        slots, sources = ring_gather(out_proj, cycle)
        partner_slots = [swap_cores(s) for s in slots]
        chip_rows = CORES * out_proj.shape[0]
        full_proj = jnp.concatenate(
            [in_core_order(m, t, first_core) for m, t in zip(slots, partner_slots)], 0
        )

        def slot_columns(rows_of_context):
            return jnp.concatenate(
                [lax.dynamic_slice_in_dim(rows_of_context, s * chip_rows, chip_rows, 1) for s in sources], 1
            )

    else:
        full_proj = lax.all_gather(out_proj, SEQ, axis=0, tiled=True)

        def slot_columns(rows_of_context):
            return rows_of_context
    score_count = SCORE_DEV
    stride = token_rows // score_count
    scored_residual = gather_rows(residual.reshape(score_count, stride, width)[:, stride - 1, :])

    seg_cols = jnp.broadcast_to(segment_ids.astype(jnp.bfloat16)[:, None], (token_rows, SEG_LANES))
    own = jnp.concatenate([joined_keys_values, seg_cols], 1)
    key_value_pair, key_seg = halo_window(own, kv_width, blocks, first_core)
    count_of_keys = key_value_pair.shape[0]
    query_pos = first_row + jnp.arange(token_rows, dtype=jnp.int32)
    key_pos = first_row - blocks * token_rows + jnp.arange(count_of_keys, dtype=jnp.int32)
    allowed = (segment_ids[:, None] == key_seg[None, :]) & (key_pos[None, :] >= 0)
    allowed = (
        allowed
        & (key_pos[None, :] <= query_pos[:, None])
        & (key_pos[None, :] > query_pos[:, None] - ATTENTION_SPAN)
    )
    heads_for_queries = queries.reshape(token_rows, KEY_VALUE_HEADS, queries_per_group, HEAD_SIZE)
    heads_for_keys = key_value_pair[:, : KEY_VALUE_HEADS * HEAD_SIZE].reshape(
        count_of_keys, KEY_VALUE_HEADS, HEAD_SIZE
    )
    heads_for_values = key_value_pair[:, KEY_VALUE_HEADS * HEAD_SIZE :].reshape(
        count_of_keys, KEY_VALUE_HEADS, HEAD_SIZE
    )
    scores = (
        jnp.einsum(
            "qhgd,khd->hgqk", heads_for_queries, heads_for_keys, preferred_element_type=jnp.float32
        )
        * score_scale
    )
    scores = jnp.where(allowed[None, None, :, :], scores, masked_score)
    row_max = jnp.max(scores, axis=-1, keepdims=True)
    raised = jnp.exp(scores - row_max)
    weights = (raised / jnp.sum(raised, axis=-1, keepdims=True)).astype(jnp.bfloat16)
    context = jnp.einsum(
        "hgqk,khd->qhgd", weights, heads_for_values, preferred_element_type=jnp.float32
    )
    context = context.reshape(token_rows, QUERY_HEADS * HEAD_SIZE).astype(jnp.bfloat16)

    scored_context = gather_rows(context.reshape(score_count, stride, -1)[:, stride - 1, :])
    picked = scored_residual.astype(jnp.float32) + jnp.dot(
        slot_columns(scored_context), full_proj, preferred_element_type=jnp.float32
    )
    normed = normalize(picked, norm_gain)
    projected = jnp.dot(slot_columns(context), full_proj, preferred_element_type=jnp.float32)
    hidden = residual.astype(jnp.float32) + projected
    layer_out = hidden.astype(jnp.bfloat16)
    logits = lax.dot_general(
        normed,
        head_weight,
        (((1,), (1,)), ((), ())),
        preferred_element_type=jnp.float32,
    )
    vocab_width = head_weight.shape[0]
    local_ids = next_ids - my_index * vocab_width
    vocab_ids = jnp.arange(vocab_width, dtype=jnp.int32)
    shard_max = jnp.max(logits, axis=1)
    shard_total = jnp.sum(jnp.exp(logits - shard_max[:, None]), axis=1)
    shard_pick = jnp.sum(jnp.where(local_ids[:, None] == vocab_ids[None, :], logits, 0.0), axis=1)
    stats = gather_rows(jnp.stack([shard_max, shard_total, shard_pick], 0))
    stats = stats.reshape(-1, 3, shard_max.shape[0])
    all_max, all_total, all_pick = stats[:, 0], stats[:, 1], stats[:, 2]
    global_max = jnp.max(all_max, axis=0)
    global_total = jnp.sum(all_total * jnp.exp(all_max - global_max[None, :]), axis=0)
    log_total = global_max + jnp.log(global_total)
    log_probs = logits - log_total[:, None]
    target_all = jnp.sum(all_pick, axis=0) - log_total
    target_logp = lax.dynamic_slice_in_dim(target_all, my_index * score_count, score_count, 0)
    return (layer_out, log_probs, target_logp)


def solution(mesh):
    parts, seq = mesh.shape["parts"], mesh.shape["seq"]
    devices = np.asarray(mesh.devices).reshape(parts, seq // CORES, CORES)
    fine = Mesh(devices, ("parts",) + SEQ)
    rows = ("parts",) + SEQ
    in_specs = (
        P(rows, None),
        P(rows, None),
        P(rows),
        P(rows, None),
        P(),
        P(SEQ, None),
        P(SEQ, None),
        P("parts"),
    )
    out_specs = (P(rows, None), P("parts", SEQ), P(rows))
    cycle = chip_cycle(mesh)
    return jax.shard_map(functools.partial(local, cycle), mesh=fine, in_specs=in_specs, out_specs=out_specs, check_vma=False)
```

```python
import jax
import jax.numpy as jnp
import numpy as np
from jax import lax
from jax.sharding import Mesh
from jax.sharding import PartitionSpec as P

QUERY_HEADS = 16
KEY_VALUE_HEADS = 8
HEAD_SIZE = 128
ATTENTION_SPAN = 1024
SCORE_DEV = 4
SEG_LANES = 128
LANES = 128
CORES = 2
SEQ = ("chip", "core")


score_scale = 168.0 ** (-0.5)
masked_score = -1e30


def seq_count():
    return lax.axis_size("chip") * lax.axis_size("core")


def seq_index():
    return lax.axis_index("chip") * lax.axis_size("core") + lax.axis_index("core")


def forward_one(value):
    count = seq_count()
    return lax.ppermute(value, SEQ, [(source, source + 1) for source in range(count - 1)])


def swap_cores(value):
    return lax.ppermute(value, "core", [(0, 1), (1, 0)])


def gather_rows(value, radix=4):
    count = seq_count()
    me = seq_index()
    data = value[None]
    stride = 1
    while stride < count:
        digits = min(radix, count // stride)
        mine = (me // stride) % digits
        received = [data]
        for offset in range(1, digits):
            pairs = []
            for i in range(count):
                d = (i // stride) % digits
                pairs.append((i, i + (((d + offset) % digits) - d) * stride))
            received.append(lax.ppermute(data, SEQ, pairs))
        stacked = jnp.stack(received, 0)
        order = (mine - jnp.arange(digits)) % digits
        data = jnp.take(stacked, order, axis=0)
        data = data.reshape((digits * data.shape[1],) + data.shape[2:])
        stride *= digits
    return data.reshape((count * value.shape[0],) + value.shape[1:])


def in_core_order(mine, theirs, first):
    return jnp.where(first, jnp.concatenate([mine, theirs], 0), jnp.concatenate([theirs, mine], 0))


def shift_chips(value, chips):
    count = seq_count()
    step = chips * CORES
    return lax.ppermute(value, SEQ, [(s, s + step) for s in range(count - step)])


def across_pair(value, from_odd):
    count = seq_count()
    pairs = [(s, s ^ CORES) for s in range(count) if ((s // CORES) % 2 == 1) == from_odd]
    return lax.ppermute(value, SEQ, pairs)


def halo_window(own, kv_width, blocks, first_core):
    assert blocks == 4 * CORES
    odd = (lax.axis_index("chip") % 2) == 1
    back2 = shift_chips(own, 2)
    own_to_odd = across_pair(own, False)
    partner_own = swap_cores(own)
    back4 = shift_chips(back2, 2)
    back2_to_even = across_pair(back2, True)
    back2_to_odd = across_pair(back2, False)
    back4_to_even = across_pair(back4, True)
    back1 = jnp.where(odd, own_to_odd, back2_to_even)
    back3 = jnp.where(odd, back2_to_odd, back4_to_even)
    near = swap_cores(jnp.stack([back1, back2], 0))
    far = swap_cores(jnp.stack([back3, back4], 0))
    pieces = []
    for mine, theirs in ((back4, far[1]), (back3, far[0]), (back2, near[1]), (back1, near[0]), (own, partner_own)):
        pieces.append(in_core_order(mine, theirs, first_core))
    sequence = jnp.concatenate(pieces, 0)
    token_rows = own.shape[0]
    core = lax.axis_index("core")
    window = lax.dynamic_slice_in_dim(sequence, core * token_rows, (blocks + 1) * token_rows, 0)
    return window[:, :kv_width], window[:, kv_width].astype(jnp.int32)


def normalize(hidden, norm_gain):
    mean_square = jnp.mean(hidden * hidden, axis=1, keepdims=True)
    return (hidden * lax.rsqrt(mean_square + 1e-06) * norm_gain[None, :]).astype(jnp.bfloat16)


def local(
    queries, joined_keys_values, segment_ids, residual, norm_gain, out_proj, head_weight, next_ids
):
    token_rows = queries.shape[0]
    blocks = ATTENTION_SPAN // token_rows
    queries_per_group = QUERY_HEADS // KEY_VALUE_HEADS
    kv_width = joined_keys_values.shape[1]
    width = residual.shape[1]
    my_index = seq_index()
    core = lax.axis_index("core")
    first_core = core == 0
    first_row = my_index * token_rows

    full_proj = lax.all_gather(out_proj, SEQ, axis=0, tiled=True)
    score_count = SCORE_DEV
    stride = token_rows // score_count
    scored_residual = gather_rows(residual.reshape(score_count, stride, width)[:, stride - 1, :])

    seg_cols = jnp.broadcast_to(segment_ids.astype(jnp.bfloat16)[:, None], (token_rows, SEG_LANES))
    own = jnp.concatenate([joined_keys_values, seg_cols], 1)
    key_value_pair, key_seg = halo_window(own, kv_width, blocks, first_core)
    count_of_keys = key_value_pair.shape[0]
    query_pos = first_row + jnp.arange(token_rows, dtype=jnp.int32)
    key_pos = first_row - blocks * token_rows + jnp.arange(count_of_keys, dtype=jnp.int32)
    allowed = (segment_ids[:, None] == key_seg[None, :]) & (key_pos[None, :] >= 0)
    allowed = (
        allowed
        & (key_pos[None, :] <= query_pos[:, None])
        & (key_pos[None, :] > query_pos[:, None] - ATTENTION_SPAN)
    )
    heads_for_keys = key_value_pair[:, : KEY_VALUE_HEADS * HEAD_SIZE].reshape(
        count_of_keys, KEY_VALUE_HEADS, HEAD_SIZE
    )
    heads_for_values = key_value_pair[:, KEY_VALUE_HEADS * HEAD_SIZE :].reshape(
        count_of_keys, KEY_VALUE_HEADS, HEAD_SIZE
    )

    def attend(rows_of_queries, rows_allowed):
        rows = rows_of_queries.shape[0]
        heads_for_queries = rows_of_queries.reshape(rows, KEY_VALUE_HEADS, queries_per_group, HEAD_SIZE)
        scores = (
            jnp.einsum(
                "qhgd,khd->hgqk", heads_for_queries, heads_for_keys, preferred_element_type=jnp.float32
            )
            * score_scale
        )
        scores = jnp.where(rows_allowed[None, None, :, :], scores, masked_score)
        row_max = jnp.max(scores, axis=-1, keepdims=True)
        raised = jnp.exp(scores - row_max)
        weights = (raised / jnp.sum(raised, axis=-1, keepdims=True)).astype(jnp.bfloat16)
        context = jnp.einsum(
            "hgqk,khd->qhgd", weights, heads_for_values, preferred_element_type=jnp.float32
        )
        return context.reshape(rows, QUERY_HEADS * HEAD_SIZE).astype(jnp.bfloat16)

    scored_rows = slice(stride - 1, token_rows, stride)
    scored_context = gather_rows(attend(queries[scored_rows], allowed[scored_rows]))
    context = attend(queries, allowed)

    picked = scored_residual.astype(jnp.float32) + jnp.dot(
        scored_context, full_proj, preferred_element_type=jnp.float32
    )
    normed = normalize(picked, norm_gain)
    projected = jnp.dot(context, full_proj, preferred_element_type=jnp.float32)
    hidden = residual.astype(jnp.float32) + projected
    layer_out = hidden.astype(jnp.bfloat16)
    logits = lax.dot_general(
        normed,
        head_weight,
        (((1,), (1,)), ((), ())),
        preferred_element_type=jnp.float32,
    )
    vocab_width = head_weight.shape[0]
    local_ids = next_ids - my_index * vocab_width
    vocab_ids = jnp.arange(vocab_width, dtype=jnp.int32)
    shard_max = jnp.max(logits, axis=1)
    shard_total = jnp.sum(jnp.exp(logits - shard_max[:, None]), axis=1)
    shard_pick = jnp.sum(jnp.where(local_ids[:, None] == vocab_ids[None, :], logits, 0.0), axis=1)
    stats = gather_rows(jnp.stack([shard_max, shard_total, shard_pick], 0))
    stats = stats.reshape(-1, 3, shard_max.shape[0])
    all_max, all_total, all_pick = stats[:, 0], stats[:, 1], stats[:, 2]
    global_max = jnp.max(all_max, axis=0)
    global_total = jnp.sum(all_total * jnp.exp(all_max - global_max[None, :]), axis=0)
    log_total = global_max + jnp.log(global_total)
    log_probs = logits - log_total[:, None]
    target_all = jnp.sum(all_pick, axis=0) - log_total
    target_logp = lax.dynamic_slice_in_dim(target_all, my_index * score_count, score_count, 0)
    return (layer_out, log_probs, target_logp)


def solution(mesh):
    parts, seq = mesh.shape["parts"], mesh.shape["seq"]
    devices = np.asarray(mesh.devices).reshape(parts, seq // CORES, CORES)
    fine = Mesh(devices, ("parts",) + SEQ)
    rows = ("parts",) + SEQ
    in_specs = (
        P(rows, None),
        P(rows, None),
        P(rows),
        P(rows, None),
        P(),
        P(SEQ, None),
        P(SEQ, None),
        P("parts"),
    )
    out_specs = (P(rows, None), P("parts", SEQ), P(rows))
    return jax.shard_map(local, mesh=fine, in_specs=in_specs, out_specs=out_specs, check_vma=False)
```

```python
import functools

import jax
import jax.numpy as jnp
import numpy as np
from jax import lax
from jax.sharding import Mesh
from jax.sharding import PartitionSpec as P

QUERY_HEADS = 16
KEY_VALUE_HEADS = 8
HEAD_SIZE = 128
ATTENTION_SPAN = 1024
SCORE_DEV = 4
SEG_LANES = 128
LANES = 128
CORES = 2
SEQ = ("chip", "core")
RING_CHIPS = 8


score_scale = 168.0 ** (-0.5)
masked_score = -1e30


def seq_count():
    return lax.axis_size("chip") * lax.axis_size("core")


def seq_index():
    return lax.axis_index("chip") * lax.axis_size("core") + lax.axis_index("core")


def forward_one(value):
    count = seq_count()
    return lax.ppermute(value, SEQ, [(source, source + 1) for source in range(count - 1)])


def swap_cores(value):
    return lax.ppermute(value, "core", [(0, 1), (1, 0)])


def gather_rows(value, radix=4):
    count = seq_count()
    me = seq_index()
    data = value[None]
    stride = 1
    while stride < count:
        digits = min(radix, count // stride)
        mine = (me // stride) % digits
        received = [data]
        for offset in range(1, digits):
            pairs = []
            for i in range(count):
                d = (i // stride) % digits
                pairs.append((i, i + (((d + offset) % digits) - d) * stride))
            received.append(lax.ppermute(data, SEQ, pairs))
        stacked = jnp.stack(received, 0)
        order = (mine - jnp.arange(digits)) % digits
        data = jnp.take(stacked, order, axis=0)
        data = data.reshape((digits * data.shape[1],) + data.shape[2:])
        stride *= digits
    return data.reshape((count * value.shape[0],) + value.shape[1:])


def in_core_order(mine, theirs, first):
    return jnp.where(first, jnp.concatenate([mine, theirs], 0), jnp.concatenate([theirs, mine], 0))


def shift_chips(value, chips):
    count = seq_count()
    step = chips * CORES
    return lax.ppermute(value, SEQ, [(s, s + step) for s in range(count - step)])


def across_pair(value, from_odd):
    count = seq_count()
    pairs = [(s, s ^ CORES) for s in range(count) if ((s // CORES) % 2 == 1) == from_odd]
    return lax.ppermute(value, SEQ, pairs)


def halo_window(own, kv_width, blocks, first_core):
    assert blocks == 4 * CORES
    odd = (lax.axis_index("chip") % 2) == 1
    back2 = shift_chips(own, 2)
    own_to_odd = across_pair(own, False)
    partner_own = swap_cores(own)
    back4 = shift_chips(back2, 2)
    back2_to_even = across_pair(back2, True)
    back2_to_odd = across_pair(back2, False)
    back4_to_even = across_pair(back4, True)
    back1 = jnp.where(odd, own_to_odd, back2_to_even)
    back3 = jnp.where(odd, back2_to_odd, back4_to_even)
    near = swap_cores(jnp.stack([back1, back2], 0))
    far = swap_cores(jnp.stack([back3, back4], 0))
    pieces = []
    for mine, theirs in ((back4, far[1]), (back3, far[0]), (back2, near[1]), (back1, near[0]), (own, partner_own)):
        pieces.append(in_core_order(mine, theirs, first_core))
    sequence = jnp.concatenate(pieces, 0)
    token_rows = own.shape[0]
    core = lax.axis_index("core")
    window = lax.dynamic_slice_in_dim(sequence, core * token_rows, (blocks + 1) * token_rows, 0)
    return window[:, :kv_width], window[:, kv_width].astype(jnp.int32)


def chip_cycle(mesh):
    chips = mesh.shape["seq"] // CORES
    try:
        coords = [tuple(d.coords) for d in np.asarray(mesh.devices)[0, ::CORES]]
        moving = [a for a in range(len(coords[0])) if coords[0][a] != coords[1][a]][0]
        fast = 1
        while fast < chips and coords[fast][moving] != coords[0][moving]:
            fast += 1
    except Exception:
        fast = 2
    slow = chips // fast
    if chips % fast or (slow % 2 and fast % 2) or fast < 2:
        return list(range(chips))
    if slow % 2:
        path = [c for c in range(fast)]
        for c in range(fast - 1, -1, -1):
            rows = range(1, slow) if (fast - 1 - c) % 2 == 0 else range(slow - 1, 0, -1)
            path += [r * fast + c for r in rows]
        return path
    path = [r * fast for r in range(slow)]
    for r in range(slow - 1, -1, -1):
        cols = range(1, fast) if (slow - 1 - r) % 2 == 0 else range(fast - 1, 0, -1)
        path += [r * fast + c for c in cols]
    return path


def ring_gather(piece, cycle):
    chips = len(cycle)
    count = seq_count()
    position = [0] * chips
    for p, k in enumerate(cycle):
        position[k] = p
    ahead = {k: cycle[(position[k] + 1) % chips] for k in range(chips)}
    behind = {k: cycle[(position[k] - 1) % chips] for k in range(chips)}
    forward = [(s, ahead[s // CORES] * CORES + s % CORES) for s in range(count)]
    backward = [(s, behind[s // CORES] * CORES + s % CORES) for s in range(count)]
    me = jnp.asarray(position, jnp.int32)[lax.axis_index("chip")]
    order = jnp.asarray(cycle, jnp.int32)
    slots, sources = [piece], [order[me]]
    current = piece
    for step in range(1, chips // 2 + 1):
        current = lax.ppermute(current, SEQ, forward)
        slots.append(current)
        sources.append(order[(me - step) % chips])
    current = piece
    for step in range(1, (chips - 1) // 2 + 1):
        current = lax.ppermute(current, SEQ, backward)
        slots.append(current)
        sources.append(order[(me + step) % chips])
    return slots, sources


def normalize(hidden, norm_gain):
    mean_square = jnp.mean(hidden * hidden, axis=1, keepdims=True)
    return (hidden * lax.rsqrt(mean_square + 1e-06) * norm_gain[None, :]).astype(jnp.bfloat16)


def local(
    cycle,
    queries, joined_keys_values, segment_ids, residual, norm_gain, out_proj, head_weight, next_ids
):
    token_rows = queries.shape[0]
    blocks = ATTENTION_SPAN // token_rows
    queries_per_group = QUERY_HEADS // KEY_VALUE_HEADS
    kv_width = joined_keys_values.shape[1]
    width = residual.shape[1]
    my_index = seq_index()
    core = lax.axis_index("core")
    first_core = core == 0
    first_row = my_index * token_rows

    if len(cycle) <= RING_CHIPS:
        slots, sources = ring_gather(out_proj, cycle)
        partner_slots = [swap_cores(s) for s in slots]
        shard_rows = out_proj.shape[0]
        full_proj = jnp.concatenate(slots + partner_slots, 0)
        shards = [s * CORES + core for s in sources] + [s * CORES + (1 - core) for s in sources]

        def slot_columns(rows_of_context):
            return jnp.concatenate(
                [lax.dynamic_slice_in_dim(rows_of_context, s * shard_rows, shard_rows, 1) for s in shards], 1
            )

    else:
        full_proj = lax.all_gather(out_proj, SEQ, axis=0, tiled=True)

        def slot_columns(rows_of_context):
            return rows_of_context
    score_count = SCORE_DEV
    stride = token_rows // score_count
    scored_residual = gather_rows(residual.reshape(score_count, stride, width)[:, stride - 1, :])

    seg_cols = jnp.broadcast_to(segment_ids.astype(jnp.bfloat16)[:, None], (token_rows, SEG_LANES))
    own = jnp.concatenate([joined_keys_values, seg_cols], 1)
    key_value_pair, key_seg = halo_window(own, kv_width, blocks, first_core)
    key_value_pair, queries, full_proj = lax.optimization_barrier((key_value_pair, queries, full_proj))
    count_of_keys = key_value_pair.shape[0]
    query_pos = first_row + jnp.arange(token_rows, dtype=jnp.int32)
    key_pos = first_row - blocks * token_rows + jnp.arange(count_of_keys, dtype=jnp.int32)
    allowed = (segment_ids[:, None] == key_seg[None, :]) & (key_pos[None, :] >= 0)
    allowed = (
        allowed
        & (key_pos[None, :] <= query_pos[:, None])
        & (key_pos[None, :] > query_pos[:, None] - ATTENTION_SPAN)
    )
    heads_for_queries = queries.reshape(token_rows, KEY_VALUE_HEADS, queries_per_group, HEAD_SIZE)
    heads_for_keys = key_value_pair[:, : KEY_VALUE_HEADS * HEAD_SIZE].reshape(
        count_of_keys, KEY_VALUE_HEADS, HEAD_SIZE
    )
    heads_for_values = key_value_pair[:, KEY_VALUE_HEADS * HEAD_SIZE :].reshape(
        count_of_keys, KEY_VALUE_HEADS, HEAD_SIZE
    )
    scores = (
        jnp.einsum(
            "qhgd,khd->hgqk", heads_for_queries, heads_for_keys, preferred_element_type=jnp.float32
        )
        * score_scale
    )
    scores = jnp.where(allowed[None, None, :, :], scores, masked_score)
    row_max = jnp.max(scores, axis=-1, keepdims=True)
    raised = jnp.exp(scores - row_max)
    weights = (raised / jnp.sum(raised, axis=-1, keepdims=True)).astype(jnp.bfloat16)
    context = jnp.einsum(
        "hgqk,khd->qhgd", weights, heads_for_values, preferred_element_type=jnp.float32
    )
    context = context.reshape(token_rows, QUERY_HEADS * HEAD_SIZE).astype(jnp.bfloat16)

    scored_context = gather_rows(context.reshape(score_count, stride, -1)[:, stride - 1, :])
    picked = scored_residual.astype(jnp.float32) + jnp.dot(
        slot_columns(scored_context), full_proj, preferred_element_type=jnp.float32
    )
    normed = normalize(picked, norm_gain)
    projected = jnp.dot(slot_columns(context), full_proj, preferred_element_type=jnp.float32)
    hidden = residual.astype(jnp.float32) + projected
    layer_out = hidden.astype(jnp.bfloat16)
    logits = lax.dot_general(
        normed,
        head_weight,
        (((1,), (1,)), ((), ())),
        preferred_element_type=jnp.float32,
    )
    vocab_width = head_weight.shape[0]
    local_ids = next_ids - my_index * vocab_width
    vocab_ids = jnp.arange(vocab_width, dtype=jnp.int32)
    shard_max = jnp.max(logits, axis=1)
    shard_total = jnp.sum(jnp.exp(logits - shard_max[:, None]), axis=1)
    shard_pick = jnp.sum(jnp.where(local_ids[:, None] == vocab_ids[None, :], logits, 0.0), axis=1)
    stats = gather_rows(jnp.stack([shard_max, shard_total, shard_pick], 0))
    stats = stats.reshape(-1, 3, shard_max.shape[0])
    all_max, all_total, all_pick = stats[:, 0], stats[:, 1], stats[:, 2]
    global_max = jnp.max(all_max, axis=0)
    global_total = jnp.sum(all_total * jnp.exp(all_max - global_max[None, :]), axis=0)
    log_total = global_max + jnp.log(global_total)
    log_probs = logits - log_total[:, None]
    target_all = jnp.sum(all_pick, axis=0) - log_total
    target_logp = lax.dynamic_slice_in_dim(target_all, my_index * score_count, score_count, 0)
    return (layer_out, log_probs, target_logp)


def solution(mesh):
    parts, seq = mesh.shape["parts"], mesh.shape["seq"]
    devices = np.asarray(mesh.devices).reshape(parts, seq // CORES, CORES)
    fine = Mesh(devices, ("parts",) + SEQ)
    rows = ("parts",) + SEQ
    in_specs = (
        P(rows, None),
        P(rows, None),
        P(rows),
        P(rows, None),
        P(),
        P(SEQ, None),
        P(SEQ, None),
        P("parts"),
    )
    out_specs = (P(rows, None), P("parts", SEQ), P(rows))
    cycle = chip_cycle(mesh)
    return jax.shard_map(functools.partial(local, cycle), mesh=fine, in_specs=in_specs, out_specs=out_specs, check_vma=False)
```

```python
import jax
import jax.numpy as jnp
import numpy as np
from jax import lax
from jax.sharding import Mesh
from jax.sharding import PartitionSpec as P

QUERY_HEADS = 16
KEY_VALUE_HEADS = 8
HEAD_SIZE = 128
ATTENTION_SPAN = 1024
SCORE_DEV = 4
DOCS = 4
LANES = 128
CORES = 2
SEQ = ("chip", "core")


score_scale = 168.0 ** (-0.5)
masked_score = -1e30


def seq_count():
    return lax.axis_size("chip") * lax.axis_size("core")


def seq_index():
    return lax.axis_index("chip") * lax.axis_size("core") + lax.axis_index("core")


def forward_one(value):
    count = seq_count()
    return lax.ppermute(value, SEQ, [(source, source + 1) for source in range(count - 1)])


def swap_cores(value):
    return lax.ppermute(value, "core", [(0, 1), (1, 0)])


def gather_rows(value, radix=4):
    count = seq_count()
    me = seq_index()
    data = value[None]
    stride = 1
    while stride < count:
        digits = min(radix, count // stride)
        mine = (me // stride) % digits
        received = [data]
        for offset in range(1, digits):
            pairs = []
            for i in range(count):
                d = (i // stride) % digits
                pairs.append((i, i + (((d + offset) % digits) - d) * stride))
            received.append(lax.ppermute(data, SEQ, pairs))
        stacked = jnp.stack(received, 0)
        order = (mine - jnp.arange(digits)) % digits
        data = jnp.take(stacked, order, axis=0)
        data = data.reshape((digits * data.shape[1],) + data.shape[2:])
        stride *= digits
    return data.reshape((count * value.shape[0],) + value.shape[1:])


def in_core_order(mine, theirs, first):
    return jnp.where(first, jnp.concatenate([mine, theirs], 0), jnp.concatenate([theirs, mine], 0))


def shift_chips(value, chips):
    count = seq_count()
    step = chips * CORES
    return lax.ppermute(value, SEQ, [(s, s + step) for s in range(count - step)])


def across_pair(value, from_odd):
    count = seq_count()
    pairs = [(s, s ^ CORES) for s in range(count) if ((s // CORES) % 2 == 1) == from_odd]
    return lax.ppermute(value, SEQ, pairs)


def halo_window(own, blocks, first_core):
    assert blocks == 4 * CORES
    odd = (lax.axis_index("chip") % 2) == 1
    back2 = shift_chips(own, 2)
    own_to_odd = across_pair(own, False)
    partner_own = swap_cores(own)
    back4 = shift_chips(back2, 2)
    back2_to_even = across_pair(back2, True)
    back2_to_odd = across_pair(back2, False)
    back4_to_even = across_pair(back4, True)
    back1 = jnp.where(odd, own_to_odd, back2_to_even)
    back3 = jnp.where(odd, back2_to_odd, back4_to_even)
    near = swap_cores(jnp.stack([back1, back2], 0))
    far = swap_cores(jnp.stack([back3, back4], 0))
    pieces = []
    for mine, theirs in ((back4, far[1]), (back3, far[0]), (back2, near[1]), (back1, near[0]), (own, partner_own)):
        pieces.append(in_core_order(mine, theirs, first_core))
    sequence = jnp.concatenate(pieces, 0)
    token_rows = own.shape[0]
    core = lax.axis_index("core")
    window = lax.dynamic_slice_in_dim(sequence, core * token_rows, (blocks + 1) * token_rows, 0)
    return window


def normalize(hidden, norm_gain):
    mean_square = jnp.mean(hidden * hidden, axis=1, keepdims=True)
    return (hidden * lax.rsqrt(mean_square + 1e-06) * norm_gain[None, :]).astype(jnp.bfloat16)


def local(
    queries, joined_keys_values, segment_ids, residual, norm_gain, out_proj, head_weight, next_ids
):
    token_rows = queries.shape[0]
    blocks = ATTENTION_SPAN // token_rows
    queries_per_group = QUERY_HEADS // KEY_VALUE_HEADS
    kv_width = joined_keys_values.shape[1]
    width = residual.shape[1]
    my_index = seq_index()
    core = lax.axis_index("core")
    first_core = core == 0
    first_row = my_index * token_rows

    full_proj = lax.all_gather(out_proj, SEQ, axis=0, tiled=True)
    score_count = SCORE_DEV
    stride = token_rows // score_count
    scored_residual = gather_rows(residual.reshape(score_count, stride, width)[:, stride - 1, :])

    values = jnp.arange(DOCS, dtype=jnp.int32)
    here = first_row + jnp.arange(token_rows, dtype=jnp.int32)
    first_seen = jnp.min(
        jnp.where(segment_ids[None, :] == values[:, None], here[None, :], jnp.iinfo(jnp.int32).max), axis=1
    )
    segment_start = jnp.min(gather_rows(first_seen).reshape(-1, DOCS), axis=0)
    first_segment = segment_ids[0]
    first_start = jnp.take(segment_start, first_segment)
    key_value_pair = halo_window(joined_keys_values, blocks, first_core)
    count_of_keys = key_value_pair.shape[0]
    rim_rows = blocks * token_rows
    query_pos = here
    key_pos = first_row - rim_rows + jnp.arange(count_of_keys, dtype=jnp.int32)
    rim_same = (segment_ids[:, None] == first_segment) & (key_pos[None, :rim_rows] >= first_start)
    own_same = segment_ids[:, None] == segment_ids[None, :]
    allowed = jnp.concatenate([rim_same, own_same], 1) & (key_pos[None, :] >= 0)
    allowed = (
        allowed
        & (key_pos[None, :] <= query_pos[:, None])
        & (key_pos[None, :] > query_pos[:, None] - ATTENTION_SPAN)
    )
    heads_for_queries = queries.reshape(token_rows, KEY_VALUE_HEADS, queries_per_group, HEAD_SIZE)
    heads_for_keys = key_value_pair[:, : KEY_VALUE_HEADS * HEAD_SIZE].reshape(
        count_of_keys, KEY_VALUE_HEADS, HEAD_SIZE
    )
    heads_for_values = key_value_pair[:, KEY_VALUE_HEADS * HEAD_SIZE :].reshape(
        count_of_keys, KEY_VALUE_HEADS, HEAD_SIZE
    )
    scores = (
        jnp.einsum(
            "qhgd,khd->hgqk", heads_for_queries, heads_for_keys, preferred_element_type=jnp.float32
        )
        * score_scale
    )
    scores = jnp.where(allowed[None, None, :, :], scores, masked_score)
    row_max = jnp.max(scores, axis=-1, keepdims=True)
    raised = jnp.exp(scores - row_max)
    weights = (raised / jnp.sum(raised, axis=-1, keepdims=True)).astype(jnp.bfloat16)
    context = jnp.einsum(
        "hgqk,khd->qhgd", weights, heads_for_values, preferred_element_type=jnp.float32
    )
    context = context.reshape(token_rows, QUERY_HEADS * HEAD_SIZE).astype(jnp.bfloat16)

    scored_context = gather_rows(context.reshape(score_count, stride, -1)[:, stride - 1, :])
    picked = scored_residual.astype(jnp.float32) + jnp.dot(
        scored_context, full_proj, preferred_element_type=jnp.float32
    )
    normed = normalize(picked, norm_gain)
    projected = jnp.dot(context, full_proj, preferred_element_type=jnp.float32)
    hidden = residual.astype(jnp.float32) + projected
    layer_out = hidden.astype(jnp.bfloat16)
    logits = lax.dot_general(
        normed,
        head_weight,
        (((1,), (1,)), ((), ())),
        preferred_element_type=jnp.float32,
    )
    vocab_width = head_weight.shape[0]
    local_ids = next_ids - my_index * vocab_width
    vocab_ids = jnp.arange(vocab_width, dtype=jnp.int32)
    shard_max = jnp.max(logits, axis=1)
    shard_total = jnp.sum(jnp.exp(logits - shard_max[:, None]), axis=1)
    shard_pick = jnp.sum(jnp.where(local_ids[:, None] == vocab_ids[None, :], logits, 0.0), axis=1)
    stats = gather_rows(jnp.stack([shard_max, shard_total, shard_pick], 0))
    stats = stats.reshape(-1, 3, shard_max.shape[0])
    all_max, all_total, all_pick = stats[:, 0], stats[:, 1], stats[:, 2]
    global_max = jnp.max(all_max, axis=0)
    global_total = jnp.sum(all_total * jnp.exp(all_max - global_max[None, :]), axis=0)
    log_total = global_max + jnp.log(global_total)
    log_probs = logits - log_total[:, None]
    target_all = jnp.sum(all_pick, axis=0) - log_total
    target_logp = lax.dynamic_slice_in_dim(target_all, my_index * score_count, score_count, 0)
    return (layer_out, log_probs, target_logp)


def solution(mesh):
    parts, seq = mesh.shape["parts"], mesh.shape["seq"]
    devices = np.asarray(mesh.devices).reshape(parts, seq // CORES, CORES)
    fine = Mesh(devices, ("parts",) + SEQ)
    rows = ("parts",) + SEQ
    in_specs = (
        P(rows, None),
        P(rows, None),
        P(rows),
        P(rows, None),
        P(),
        P(SEQ, None),
        P(SEQ, None),
        P("parts"),
    )
    out_specs = (P(rows, None), P("parts", SEQ), P(rows))
    return jax.shard_map(local, mesh=fine, in_specs=in_specs, out_specs=out_specs, check_vma=False)
```

```python
import jax
import jax.numpy as jnp
import numpy as np
from jax import lax
from jax.sharding import Mesh
from jax.sharding import PartitionSpec as P

QUERY_HEADS = 16
KEY_VALUE_HEADS = 8
HEAD_SIZE = 128
ATTENTION_SPAN = 1024
SCORE_DEV = 4
SEG_LANES = 128
LANES = 128
CORES = 2
SEQ = ("chip", "core")


score_scale = 168.0 ** (-0.5)
masked_score = -1e30


def seq_count():
    return lax.axis_size("chip") * lax.axis_size("core")


def seq_index():
    return lax.axis_index("chip") * lax.axis_size("core") + lax.axis_index("core")


def forward_one(value):
    count = seq_count()
    return lax.ppermute(value, SEQ, [(source, source + 1) for source in range(count - 1)])


def swap_cores(value):
    return lax.ppermute(value, "core", [(0, 1), (1, 0)])


def gather_rows(value, radix=4):
    count = seq_count()
    me = seq_index()
    data = value[None]
    stride = 1
    while stride < count:
        digits = min(radix, count // stride)
        mine = (me // stride) % digits
        received = [data]
        for offset in range(1, digits):
            pairs = []
            for i in range(count):
                d = (i // stride) % digits
                pairs.append((i, i + (((d + offset) % digits) - d) * stride))
            received.append(lax.ppermute(data, SEQ, pairs))
        stacked = jnp.stack(received, 0)
        order = (mine - jnp.arange(digits)) % digits
        data = jnp.take(stacked, order, axis=0)
        data = data.reshape((digits * data.shape[1],) + data.shape[2:])
        stride *= digits
    return data.reshape((count * value.shape[0],) + value.shape[1:])


def in_core_order(mine, theirs, first):
    return jnp.where(first, jnp.concatenate([mine, theirs], 0), jnp.concatenate([theirs, mine], 0))


def shift_chips(value, chips):
    count = seq_count()
    step = chips * CORES
    return lax.ppermute(value, SEQ, [(s, s + step) for s in range(count - step)])


def across_pair(value, from_odd):
    count = seq_count()
    pairs = [(s, s ^ CORES) for s in range(count) if ((s // CORES) % 2 == 1) == from_odd]
    return lax.ppermute(value, SEQ, pairs)


def halo_window(own, kv_width, blocks, first_core):
    assert blocks == 4 * CORES
    odd = (lax.axis_index("chip") % 2) == 1
    back2 = shift_chips(own, 2)
    own_to_odd = across_pair(own, False)
    partner_own = swap_cores(own)
    back4 = shift_chips(back2, 2)
    back2_to_even = across_pair(back2, True)
    back2_to_odd = across_pair(back2, False)
    back4_to_even = across_pair(back4, True)
    back1 = jnp.where(odd, own_to_odd, back2_to_even)
    back3 = jnp.where(odd, back2_to_odd, back4_to_even)
    near = swap_cores(jnp.stack([back1, back2], 0))
    far = swap_cores(jnp.stack([back3, back4], 0))
    pieces = []
    for mine, theirs in ((back4, far[1]), (back3, far[0]), (back2, near[1]), (back1, near[0]), (own, partner_own)):
        pieces.append(in_core_order(mine, theirs, first_core))
    sequence = jnp.concatenate(pieces, 0)
    token_rows = own.shape[0]
    core = lax.axis_index("core")
    window = lax.dynamic_slice_in_dim(sequence, core * token_rows, (blocks + 1) * token_rows, 0)
    return window[:, :kv_width], window[:, kv_width].astype(jnp.int32)


def normalize(hidden, norm_gain):
    mean_square = jnp.mean(hidden * hidden, axis=1, keepdims=True)
    return (hidden * lax.rsqrt(mean_square + 1e-06) * norm_gain[None, :]).astype(jnp.bfloat16)


def local(
    queries, joined_keys_values, segment_ids, residual, norm_gain, out_proj, head_weight, next_ids
):
    token_rows = queries.shape[0]
    blocks = ATTENTION_SPAN // token_rows
    queries_per_group = QUERY_HEADS // KEY_VALUE_HEADS
    kv_width = joined_keys_values.shape[1]
    width = residual.shape[1]
    my_index = seq_index()
    core = lax.axis_index("core")
    first_core = core == 0
    first_row = my_index * token_rows

    full_proj = lax.all_gather(out_proj, SEQ, axis=0, tiled=True)
    score_count = SCORE_DEV
    stride = token_rows // score_count

    seg_cols = jnp.broadcast_to(segment_ids.astype(jnp.bfloat16)[:, None], (token_rows, SEG_LANES))
    own = jnp.concatenate([joined_keys_values, seg_cols], 1)
    key_value_pair, key_seg = halo_window(own, kv_width, blocks, first_core)
    count_of_keys = key_value_pair.shape[0]
    query_pos = first_row + jnp.arange(token_rows, dtype=jnp.int32)
    key_pos = first_row - blocks * token_rows + jnp.arange(count_of_keys, dtype=jnp.int32)
    allowed = (segment_ids[:, None] == key_seg[None, :]) & (key_pos[None, :] >= 0)
    allowed = (
        allowed
        & (key_pos[None, :] <= query_pos[:, None])
        & (key_pos[None, :] > query_pos[:, None] - ATTENTION_SPAN)
    )
    heads_for_queries = queries.reshape(token_rows, KEY_VALUE_HEADS, queries_per_group, HEAD_SIZE)
    heads_for_keys = key_value_pair[:, : KEY_VALUE_HEADS * HEAD_SIZE].reshape(
        count_of_keys, KEY_VALUE_HEADS, HEAD_SIZE
    )
    heads_for_values = key_value_pair[:, KEY_VALUE_HEADS * HEAD_SIZE :].reshape(
        count_of_keys, KEY_VALUE_HEADS, HEAD_SIZE
    )
    scores = (
        jnp.einsum(
            "qhgd,khd->hgqk", heads_for_queries, heads_for_keys, preferred_element_type=jnp.float32
        )
        * score_scale
    )
    scores = jnp.where(allowed[None, None, :, :], scores, masked_score)
    row_max = jnp.max(scores, axis=-1, keepdims=True)
    raised = jnp.exp(scores - row_max)
    weights = (raised / jnp.sum(raised, axis=-1, keepdims=True)).astype(jnp.bfloat16)
    context = jnp.einsum(
        "hgqk,khd->qhgd", weights, heads_for_values, preferred_element_type=jnp.float32
    )
    context = context.reshape(token_rows, QUERY_HEADS * HEAD_SIZE).astype(jnp.bfloat16)

    scored = gather_rows(
        jnp.concatenate(
            [
                context.reshape(score_count, stride, -1)[:, stride - 1, :],
                residual.reshape(score_count, stride, width)[:, stride - 1, :],
            ],
            1,
        )
    )
    context_width = context.shape[1]
    scored_context, scored_residual = scored[:, :context_width], scored[:, context_width:]
    picked = scored_residual.astype(jnp.float32) + jnp.dot(
        scored_context, full_proj, preferred_element_type=jnp.float32
    )
    normed = normalize(picked, norm_gain)
    projected = jnp.dot(context, full_proj, preferred_element_type=jnp.float32)
    hidden = residual.astype(jnp.float32) + projected
    layer_out = hidden.astype(jnp.bfloat16)
    logits = lax.dot_general(
        normed,
        head_weight,
        (((1,), (1,)), ((), ())),
        preferred_element_type=jnp.float32,
    )
    vocab_width = head_weight.shape[0]
    local_ids = next_ids - my_index * vocab_width
    vocab_ids = jnp.arange(vocab_width, dtype=jnp.int32)
    shard_max = jnp.max(logits, axis=1)
    shard_total = jnp.sum(jnp.exp(logits - shard_max[:, None]), axis=1)
    shard_pick = jnp.sum(jnp.where(local_ids[:, None] == vocab_ids[None, :], logits, 0.0), axis=1)
    stats = gather_rows(jnp.stack([shard_max, shard_total, shard_pick], 0))
    stats = stats.reshape(-1, 3, shard_max.shape[0])
    all_max, all_total, all_pick = stats[:, 0], stats[:, 1], stats[:, 2]
    global_max = jnp.max(all_max, axis=0)
    global_total = jnp.sum(all_total * jnp.exp(all_max - global_max[None, :]), axis=0)
    log_total = global_max + jnp.log(global_total)
    log_probs = logits - log_total[:, None]
    target_all = jnp.sum(all_pick, axis=0) - log_total
    target_logp = lax.dynamic_slice_in_dim(target_all, my_index * score_count, score_count, 0)
    return (layer_out, log_probs, target_logp)


def solution(mesh):
    parts, seq = mesh.shape["parts"], mesh.shape["seq"]
    devices = np.asarray(mesh.devices).reshape(parts, seq // CORES, CORES)
    fine = Mesh(devices, ("parts",) + SEQ)
    rows = ("parts",) + SEQ
    in_specs = (
        P(rows, None),
        P(rows, None),
        P(rows),
        P(rows, None),
        P(),
        P(SEQ, None),
        P(SEQ, None),
        P("parts"),
    )
    out_specs = (P(rows, None), P("parts", SEQ), P(rows))
    return jax.shard_map(local, mesh=fine, in_specs=in_specs, out_specs=out_specs, check_vma=False)
```

```python
import jax
import jax.numpy as jnp
import numpy as np
from jax import lax
from jax.sharding import Mesh
from jax.sharding import PartitionSpec as P

QUERY_HEADS = 16
KEY_VALUE_HEADS = 8
HEAD_SIZE = 128
ATTENTION_SPAN = 1024
SCORE_DEV = 4
SEG_LANES = 128
LANES = 128
CORES = 2
SEQ = ("chip", "core")


score_scale = 168.0 ** (-0.5)
masked_score = -1e30


def seq_count():
    return lax.axis_size("chip") * lax.axis_size("core")


def seq_index():
    return lax.axis_index("chip") * lax.axis_size("core") + lax.axis_index("core")


def forward_one(value):
    count = seq_count()
    return lax.ppermute(value, SEQ, [(source, source + 1) for source in range(count - 1)])


def swap_cores(value):
    return lax.ppermute(value, "core", [(0, 1), (1, 0)])


def gather_rows(value, radix=4):
    count = seq_count()
    me = seq_index()
    data = value[None]
    stride = 1
    while stride < count:
        digits = min(radix, count // stride)
        mine = (me // stride) % digits
        received = [data]
        for offset in range(1, digits):
            pairs = []
            for i in range(count):
                d = (i // stride) % digits
                pairs.append((i, i + (((d + offset) % digits) - d) * stride))
            received.append(lax.ppermute(data, SEQ, pairs))
        stacked = jnp.stack(received, 0)
        order = (mine - jnp.arange(digits)) % digits
        data = jnp.take(stacked, order, axis=0)
        data = data.reshape((digits * data.shape[1],) + data.shape[2:])
        stride *= digits
    return data.reshape((count * value.shape[0],) + value.shape[1:])


def in_core_order(mine, theirs, first):
    return jnp.where(first, jnp.concatenate([mine, theirs], 0), jnp.concatenate([theirs, mine], 0))


def shift_chips(value, chips):
    count = seq_count()
    step = chips * CORES
    return lax.ppermute(value, SEQ, [(s, s + step) for s in range(count - step)])


def across_pair(value, from_odd):
    count = seq_count()
    pairs = [(s, s ^ CORES) for s in range(count) if ((s // CORES) % 2 == 1) == from_odd]
    return lax.ppermute(value, SEQ, pairs)


def halo_window(own, kv_width, blocks, first_core):
    assert blocks == 4 * CORES
    odd = (lax.axis_index("chip") % 2) == 1
    back2 = shift_chips(own, 2)
    own_to_odd = across_pair(own, False)
    partner_own = swap_cores(own)
    back4 = shift_chips(back2, 2)
    back2_to_even = across_pair(back2, True)
    back2_to_odd = across_pair(back2, False)
    back4_to_even = across_pair(back4, True)
    back1 = jnp.where(odd, own_to_odd, back2_to_even)
    back3 = jnp.where(odd, back2_to_odd, back4_to_even)
    near = swap_cores(jnp.stack([back1, back2], 0))
    far = swap_cores(jnp.stack([back3, back4], 0))
    pieces = []
    for mine, theirs in ((back4, far[1]), (back3, far[0]), (back2, near[1]), (back1, near[0]), (own, partner_own)):
        pieces.append(in_core_order(mine, theirs, first_core))
    sequence = jnp.concatenate(pieces, 0)
    token_rows = own.shape[0]
    core = lax.axis_index("core")
    window = lax.dynamic_slice_in_dim(sequence, core * token_rows, (blocks + 1) * token_rows, 0)
    return window[:, :kv_width], window[:, kv_width].astype(jnp.int32)


def normalize(hidden, norm_gain):
    mean_square = jnp.mean(hidden * hidden, axis=1, keepdims=True)
    return (hidden * lax.rsqrt(mean_square + 1e-06) * norm_gain[None, :]).astype(jnp.bfloat16)


def local(
    queries, joined_keys_values, segment_ids, residual, norm_gain, out_proj, head_weight, next_ids
):
    token_rows = queries.shape[0]
    blocks = ATTENTION_SPAN // token_rows
    queries_per_group = QUERY_HEADS // KEY_VALUE_HEADS
    kv_width = joined_keys_values.shape[1]
    width = residual.shape[1]
    my_index = seq_index()
    core = lax.axis_index("core")
    first_core = core == 0
    first_row = my_index * token_rows

    full_proj = lax.all_gather(out_proj, SEQ, axis=0, tiled=True)
    score_count = SCORE_DEV
    stride = token_rows // score_count
    scored_residual = gather_rows(residual.reshape(score_count, stride, width)[:, stride - 1, :])

    seg_cols = jnp.broadcast_to(segment_ids.astype(jnp.bfloat16)[:, None], (token_rows, SEG_LANES))
    own = jnp.concatenate([joined_keys_values, seg_cols], 1)
    key_value_pair, key_seg = halo_window(own, kv_width, blocks, first_core)
    count_of_keys = key_value_pair.shape[0]
    query_pos = first_row + jnp.arange(token_rows, dtype=jnp.int32)
    key_pos = first_row - blocks * token_rows + jnp.arange(count_of_keys, dtype=jnp.int32)
    allowed = (segment_ids[:, None] == key_seg[None, :]) & (key_pos[None, :] >= 0)
    allowed = (
        allowed
        & (key_pos[None, :] <= query_pos[:, None])
        & (key_pos[None, :] > query_pos[:, None] - ATTENTION_SPAN)
    )
    heads_for_queries = queries.reshape(token_rows, KEY_VALUE_HEADS, queries_per_group, HEAD_SIZE)
    heads_for_keys = key_value_pair[:, : KEY_VALUE_HEADS * HEAD_SIZE].reshape(
        count_of_keys, KEY_VALUE_HEADS, HEAD_SIZE
    )
    heads_for_values = key_value_pair[:, KEY_VALUE_HEADS * HEAD_SIZE :].reshape(
        count_of_keys, KEY_VALUE_HEADS, HEAD_SIZE
    )
    scores = (
        jnp.einsum(
            "qhgd,khd->hgqk", heads_for_queries, heads_for_keys, preferred_element_type=jnp.float32
        )
        * score_scale
    )
    scores = jnp.where(allowed[None, None, :, :], scores, masked_score)
    row_max = jnp.max(scores, axis=-1, keepdims=True)
    raised = jnp.exp(scores - row_max)
    weights = (raised / jnp.sum(raised, axis=-1, keepdims=True)).astype(jnp.bfloat16)
    context = jnp.einsum(
        "hgqk,khd->qhgd", weights, heads_for_values, preferred_element_type=jnp.float32
    )
    context = context.reshape(token_rows, QUERY_HEADS * HEAD_SIZE).astype(jnp.bfloat16)

    scored_context = gather_rows(context.reshape(score_count, stride, -1)[:, stride - 1, :])
    both = jnp.dot(
        jnp.concatenate([scored_context, context], 0), full_proj, preferred_element_type=jnp.float32
    )
    scored_total = scored_context.shape[0]
    picked = scored_residual.astype(jnp.float32) + both[:scored_total]
    normed = normalize(picked, norm_gain)
    projected = both[scored_total:]
    hidden = residual.astype(jnp.float32) + projected
    layer_out = hidden.astype(jnp.bfloat16)
    logits = lax.dot_general(
        normed,
        head_weight,
        (((1,), (1,)), ((), ())),
        preferred_element_type=jnp.float32,
    )
    vocab_width = head_weight.shape[0]
    local_ids = next_ids - my_index * vocab_width
    vocab_ids = jnp.arange(vocab_width, dtype=jnp.int32)
    shard_max = jnp.max(logits, axis=1)
    shard_total = jnp.sum(jnp.exp(logits - shard_max[:, None]), axis=1)
    shard_pick = jnp.sum(jnp.where(local_ids[:, None] == vocab_ids[None, :], logits, 0.0), axis=1)
    stats = gather_rows(jnp.stack([shard_max, shard_total, shard_pick], 0))
    stats = stats.reshape(-1, 3, shard_max.shape[0])
    all_max, all_total, all_pick = stats[:, 0], stats[:, 1], stats[:, 2]
    global_max = jnp.max(all_max, axis=0)
    global_total = jnp.sum(all_total * jnp.exp(all_max - global_max[None, :]), axis=0)
    log_total = global_max + jnp.log(global_total)
    log_probs = logits - log_total[:, None]
    target_all = jnp.sum(all_pick, axis=0) - log_total
    target_logp = lax.dynamic_slice_in_dim(target_all, my_index * score_count, score_count, 0)
    return (layer_out, log_probs, target_logp)


def solution(mesh):
    parts, seq = mesh.shape["parts"], mesh.shape["seq"]
    devices = np.asarray(mesh.devices).reshape(parts, seq // CORES, CORES)
    fine = Mesh(devices, ("parts",) + SEQ)
    rows = ("parts",) + SEQ
    in_specs = (
        P(rows, None),
        P(rows, None),
        P(rows),
        P(rows, None),
        P(),
        P(SEQ, None),
        P(SEQ, None),
        P("parts"),
    )
    out_specs = (P(rows, None), P("parts", SEQ), P(rows))
    return jax.shard_map(local, mesh=fine, in_specs=in_specs, out_specs=out_specs, check_vma=False)
```

```python
import jax
import jax.numpy as jnp
import numpy as np
from jax import lax
from jax.sharding import Mesh
from jax.sharding import PartitionSpec as P

QUERY_HEADS = 16
KEY_VALUE_HEADS = 8
HEAD_SIZE = 128
ATTENTION_SPAN = 1024
SCORE_DEV = 4
SEG_LANES = 128
LANES = 128
CORES = 2
SEQ = ("chip", "core")


score_scale = 168.0 ** (-0.5)
masked_score = -1e30


def seq_count():
    return lax.axis_size("chip") * lax.axis_size("core")


def seq_index():
    return lax.axis_index("chip") * lax.axis_size("core") + lax.axis_index("core")


def forward_one(value):
    count = seq_count()
    return lax.ppermute(value, SEQ, [(source, source + 1) for source in range(count - 1)])


def swap_cores(value):
    return lax.ppermute(value, "core", [(0, 1), (1, 0)])


def gather_rows(value, radix=4):
    count = seq_count()
    me = seq_index()
    data = value[None]
    stride = 1
    while stride < count:
        digits = min(radix, count // stride)
        mine = (me // stride) % digits
        received = [data]
        for offset in range(1, digits):
            pairs = []
            for i in range(count):
                d = (i // stride) % digits
                pairs.append((i, i + (((d + offset) % digits) - d) * stride))
            received.append(lax.ppermute(data, SEQ, pairs))
        stacked = jnp.stack(received, 0)
        order = (mine - jnp.arange(digits)) % digits
        data = jnp.take(stacked, order, axis=0)
        data = data.reshape((digits * data.shape[1],) + data.shape[2:])
        stride *= digits
    return data.reshape((count * value.shape[0],) + value.shape[1:])


def in_core_order(mine, theirs, first):
    return jnp.where(first, jnp.concatenate([mine, theirs], 0), jnp.concatenate([theirs, mine], 0))


def shift_chips(value, chips):
    count = seq_count()
    step = chips * CORES
    return lax.ppermute(value, SEQ, [(s, s + step) for s in range(count - step)])


def across_pair(value, from_odd):
    count = seq_count()
    pairs = [(s, s ^ CORES) for s in range(count) if ((s // CORES) % 2 == 1) == from_odd]
    return lax.ppermute(value, SEQ, pairs)


def halo_window(own, kv_width, blocks, first_core):
    assert blocks == 4 * CORES
    odd = (lax.axis_index("chip") % 2) == 1
    back2 = shift_chips(own, 2)
    own_to_odd = across_pair(own, False)
    partner_own = swap_cores(own)
    back4 = shift_chips(back2, 2)
    back2_to_even = across_pair(back2, True)
    back2_to_odd = across_pair(back2, False)
    back4_to_even = across_pair(back4, True)
    back1 = jnp.where(odd, own_to_odd, back2_to_even)
    back3 = jnp.where(odd, back2_to_odd, back4_to_even)
    near = swap_cores(jnp.stack([back1, back2], 0))
    far = swap_cores(jnp.stack([back3, back4], 0))
    pieces = []
    for mine, theirs in ((back4, far[1]), (back3, far[0]), (back2, near[1]), (back1, near[0]), (own, partner_own)):
        pieces.append(in_core_order(mine, theirs, first_core))
    sequence = jnp.concatenate(pieces, 0)
    return sequence[:, :kv_width], sequence[:, kv_width].astype(jnp.int32)


def normalize(hidden, norm_gain):
    mean_square = jnp.mean(hidden * hidden, axis=1, keepdims=True)
    return (hidden * lax.rsqrt(mean_square + 1e-06) * norm_gain[None, :]).astype(jnp.bfloat16)


def local(
    queries, joined_keys_values, segment_ids, residual, norm_gain, out_proj, head_weight, next_ids
):
    token_rows = queries.shape[0]
    blocks = ATTENTION_SPAN // token_rows
    queries_per_group = QUERY_HEADS // KEY_VALUE_HEADS
    kv_width = joined_keys_values.shape[1]
    width = residual.shape[1]
    my_index = seq_index()
    core = lax.axis_index("core")
    first_core = core == 0
    first_row = my_index * token_rows

    full_proj = lax.all_gather(out_proj, SEQ, axis=0, tiled=True)
    score_count = SCORE_DEV
    stride = token_rows // score_count
    scored_residual = gather_rows(residual.reshape(score_count, stride, width)[:, stride - 1, :])

    seg_cols = jnp.broadcast_to(segment_ids.astype(jnp.bfloat16)[:, None], (token_rows, SEG_LANES))
    own = jnp.concatenate([joined_keys_values, seg_cols], 1)
    key_value_pair, key_seg = halo_window(own, kv_width, blocks, first_core)
    count_of_keys = key_value_pair.shape[0]
    query_pos = first_row + jnp.arange(token_rows, dtype=jnp.int32)
    key_pos = (lax.axis_index("chip") * CORES - blocks) * token_rows + jnp.arange(count_of_keys, dtype=jnp.int32)
    allowed = (segment_ids[:, None] == key_seg[None, :]) & (key_pos[None, :] >= 0)
    allowed = (
        allowed
        & (key_pos[None, :] <= query_pos[:, None])
        & (key_pos[None, :] > query_pos[:, None] - ATTENTION_SPAN)
    )
    heads_for_queries = queries.reshape(token_rows, KEY_VALUE_HEADS, queries_per_group, HEAD_SIZE)
    heads_for_keys = key_value_pair[:, : KEY_VALUE_HEADS * HEAD_SIZE].reshape(
        count_of_keys, KEY_VALUE_HEADS, HEAD_SIZE
    )
    heads_for_values = key_value_pair[:, KEY_VALUE_HEADS * HEAD_SIZE :].reshape(
        count_of_keys, KEY_VALUE_HEADS, HEAD_SIZE
    )
    scores = (
        jnp.einsum(
            "qhgd,khd->hgqk", heads_for_queries, heads_for_keys, preferred_element_type=jnp.float32
        )
        * score_scale
    )
    scores = jnp.where(allowed[None, None, :, :], scores, masked_score)
    row_max = jnp.max(scores, axis=-1, keepdims=True)
    raised = jnp.exp(scores - row_max)
    weights = (raised / jnp.sum(raised, axis=-1, keepdims=True)).astype(jnp.bfloat16)
    context = jnp.einsum(
        "hgqk,khd->qhgd", weights, heads_for_values, preferred_element_type=jnp.float32
    )
    context = context.reshape(token_rows, QUERY_HEADS * HEAD_SIZE).astype(jnp.bfloat16)

    scored_context = gather_rows(context.reshape(score_count, stride, -1)[:, stride - 1, :])
    both = jnp.dot(
        jnp.concatenate([scored_context, context], 0), full_proj, preferred_element_type=jnp.float32
    )
    scored_total = scored_context.shape[0]
    picked = scored_residual.astype(jnp.float32) + both[:scored_total]
    normed = normalize(picked, norm_gain)
    projected = both[scored_total:]
    hidden = residual.astype(jnp.float32) + projected
    layer_out = hidden.astype(jnp.bfloat16)
    logits = lax.dot_general(
        normed,
        head_weight,
        (((1,), (1,)), ((), ())),
        preferred_element_type=jnp.float32,
    )
    vocab_width = head_weight.shape[0]
    local_ids = next_ids - my_index * vocab_width
    vocab_ids = jnp.arange(vocab_width, dtype=jnp.int32)
    shard_max = jnp.max(logits, axis=1)
    shard_total = jnp.sum(jnp.exp(logits - shard_max[:, None]), axis=1)
    shard_pick = jnp.sum(jnp.where(local_ids[:, None] == vocab_ids[None, :], logits, 0.0), axis=1)
    stats = gather_rows(jnp.stack([shard_max, shard_total, shard_pick], 0))
    stats = stats.reshape(-1, 3, shard_max.shape[0])
    all_max, all_total, all_pick = stats[:, 0], stats[:, 1], stats[:, 2]
    global_max = jnp.max(all_max, axis=0)
    global_total = jnp.sum(all_total * jnp.exp(all_max - global_max[None, :]), axis=0)
    log_total = global_max + jnp.log(global_total)
    log_probs = logits - log_total[:, None]
    target_all = jnp.sum(all_pick, axis=0) - log_total
    target_logp = lax.dynamic_slice_in_dim(target_all, my_index * score_count, score_count, 0)
    return (layer_out, log_probs, target_logp)


def solution(mesh):
    parts, seq = mesh.shape["parts"], mesh.shape["seq"]
    devices = np.asarray(mesh.devices).reshape(parts, seq // CORES, CORES)
    fine = Mesh(devices, ("parts",) + SEQ)
    rows = ("parts",) + SEQ
    in_specs = (
        P(rows, None),
        P(rows, None),
        P(rows),
        P(rows, None),
        P(),
        P(SEQ, None),
        P(SEQ, None),
        P("parts"),
    )
    out_specs = (P(rows, None), P("parts", SEQ), P(rows))
    return jax.shard_map(local, mesh=fine, in_specs=in_specs, out_specs=out_specs, check_vma=False)
```

```python
import jax
import jax.numpy as jnp
import numpy as np
from jax import lax
from jax.sharding import Mesh
from jax.sharding import PartitionSpec as P

QUERY_HEADS = 16
KEY_VALUE_HEADS = 8
HEAD_SIZE = 128
ATTENTION_SPAN = 1024
SCORE_DEV = 4
SEG_LANES = 128
LANES = 128
CORES = 2
SEQ = ("chip", "core")


score_scale = 168.0 ** (-0.5)
masked_score = -1e30


def seq_count():
    return lax.axis_size("chip") * lax.axis_size("core")


def seq_index():
    return lax.axis_index("chip") * lax.axis_size("core") + lax.axis_index("core")


def forward_one(value):
    count = seq_count()
    return lax.ppermute(value, SEQ, [(source, source + 1) for source in range(count - 1)])


def swap_cores(value):
    return lax.ppermute(value, "core", [(0, 1), (1, 0)])


def gather_rows(value, radix=4):
    count = seq_count()
    me = seq_index()
    data = value[None]
    stride = 1
    while stride < count:
        digits = min(radix, count // stride)
        mine = (me // stride) % digits
        received = [data]
        for offset in range(1, digits):
            pairs = []
            for i in range(count):
                d = (i // stride) % digits
                pairs.append((i, i + (((d + offset) % digits) - d) * stride))
            received.append(lax.ppermute(data, SEQ, pairs))
        stacked = jnp.stack(received, 0)
        order = (mine - jnp.arange(digits)) % digits
        data = jnp.take(stacked, order, axis=0)
        data = data.reshape((digits * data.shape[1],) + data.shape[2:])
        stride *= digits
    return data.reshape((count * value.shape[0],) + value.shape[1:])


def in_core_order(mine, theirs, first):
    return jnp.where(first, jnp.concatenate([mine, theirs], 0), jnp.concatenate([theirs, mine], 0))


def shift_chips(value, chips):
    count = seq_count()
    step = chips * CORES
    return lax.ppermute(value, SEQ, [(s, s + step) for s in range(count - step)])


def across_pair(value, from_odd):
    count = seq_count()
    pairs = [(s, s ^ CORES) for s in range(count) if ((s // CORES) % 2 == 1) == from_odd]
    return lax.ppermute(value, SEQ, pairs)


def halo_window(own, kv_width, blocks, first_core):
    assert blocks == 4 * CORES
    odd = (lax.axis_index("chip") % 2) == 1
    back2 = shift_chips(own, 2)
    own_to_odd = across_pair(own, False)
    partner_own = swap_cores(own)
    back4 = shift_chips(back2, 2)
    back2_to_even = across_pair(back2, True)
    back2_to_odd = across_pair(back2, False)
    back4_to_even = across_pair(back4, True)
    back1 = jnp.where(odd, own_to_odd, back2_to_even)
    back3 = jnp.where(odd, back2_to_odd, back4_to_even)
    near = swap_cores(jnp.stack([back1, back2], 0))
    far = swap_cores(jnp.stack([back3, back4], 0))
    pieces = []
    for mine, theirs in ((back4, far[1]), (back3, far[0]), (back2, near[1]), (back1, near[0]), (own, partner_own)):
        pieces.append(in_core_order(mine, theirs, first_core))
    sequence = jnp.concatenate(pieces, 0)
    token_rows = own.shape[0]
    core = lax.axis_index("core")
    window = lax.dynamic_slice_in_dim(sequence, core * token_rows, (blocks + 1) * token_rows, 0)
    return window[:, :kv_width], window[:, kv_width].astype(jnp.int32)


def normalize(hidden, norm_gain):
    mean_square = jnp.mean(hidden * hidden, axis=1, keepdims=True)
    return (hidden * lax.rsqrt(mean_square + 1e-06) * norm_gain[None, :]).astype(jnp.bfloat16)


def local(
    queries, joined_keys_values, segment_ids, residual, norm_gain, out_proj, head_weight, next_ids
):
    token_rows = queries.shape[0]
    blocks = ATTENTION_SPAN // token_rows
    queries_per_group = QUERY_HEADS // KEY_VALUE_HEADS
    kv_width = joined_keys_values.shape[1]
    width = residual.shape[1]
    my_index = seq_index()
    core = lax.axis_index("core")
    first_core = core == 0
    first_row = my_index * token_rows

    full_proj = lax.all_gather(out_proj, SEQ, axis=0, tiled=True)
    score_count = SCORE_DEV
    stride = token_rows // score_count
    scored_residual = gather_rows(residual.reshape(score_count, stride, width)[:, stride - 1, :])

    seg_cols = jnp.broadcast_to(segment_ids.astype(jnp.bfloat16)[:, None], (token_rows, SEG_LANES))
    own = jnp.concatenate([joined_keys_values, seg_cols], 1)
    key_value_pair, key_seg = halo_window(own, kv_width, blocks, first_core)
    count_of_keys = key_value_pair.shape[0]
    query_pos = first_row + jnp.arange(token_rows, dtype=jnp.int32)
    key_pos = first_row - blocks * token_rows + jnp.arange(count_of_keys, dtype=jnp.int32)
    allowed = (segment_ids[:, None] == key_seg[None, :]) & (key_pos[None, :] >= 0)
    allowed = (
        allowed
        & (key_pos[None, :] <= query_pos[:, None])
        & (key_pos[None, :] > query_pos[:, None] - ATTENTION_SPAN)
    )
    heads_for_queries = queries.reshape(token_rows, KEY_VALUE_HEADS, queries_per_group, HEAD_SIZE)
    heads_for_keys = key_value_pair[:, : KEY_VALUE_HEADS * HEAD_SIZE].reshape(
        count_of_keys, KEY_VALUE_HEADS, HEAD_SIZE
    )
    heads_for_values = key_value_pair[:, KEY_VALUE_HEADS * HEAD_SIZE :].reshape(
        count_of_keys, KEY_VALUE_HEADS, HEAD_SIZE
    )
    scores = (
        jnp.einsum(
            "qhgd,khd->hgqk", heads_for_queries, heads_for_keys, preferred_element_type=jnp.float32
        )
        * score_scale
    )
    scores = jnp.where(allowed[None, None, :, :], scores, masked_score)
    row_max = jnp.max(scores, axis=-1, keepdims=True)
    raised = jnp.exp(scores - row_max)
    weights = (raised / jnp.sum(raised, axis=-1, keepdims=True)).astype(jnp.bfloat16)
    context = jnp.einsum(
        "hgqk,khd->qhgd", weights, heads_for_values, preferred_element_type=jnp.float32
    )
    context = context.reshape(token_rows, QUERY_HEADS * HEAD_SIZE).astype(jnp.bfloat16)

    scored_context = gather_rows(context.reshape(score_count, stride, -1)[:, stride - 1, :])
    both = jnp.dot(
        jnp.concatenate([scored_context, context], 0), full_proj, preferred_element_type=jnp.float32
    )
    scored_total = scored_context.shape[0]
    picked = scored_residual.astype(jnp.float32) + both[:scored_total]
    normed = normalize(picked, norm_gain)
    projected = both[scored_total:]
    hidden = residual.astype(jnp.float32) + projected
    layer_out = hidden.astype(jnp.bfloat16)
    logits = lax.dot_general(
        normed,
        head_weight,
        (((1,), (1,)), ((), ())),
        preferred_element_type=jnp.float32,
    )
    vocab_width = head_weight.shape[0]
    local_ids = next_ids - my_index * vocab_width
    vocab_ids = jnp.arange(vocab_width, dtype=jnp.int32)
    shard_max = jnp.max(logits, axis=1)
    shard_total = jnp.sum(jnp.exp(logits - shard_max[:, None]), axis=1)
    shard_pick = jnp.sum(jnp.where(local_ids[:, None] == vocab_ids[None, :], logits, 0.0), axis=1)
    stats = gather_rows(jnp.stack([shard_max, shard_total, shard_pick], 0), radix=16)
    stats = stats.reshape(-1, 3, shard_max.shape[0])
    all_max, all_total, all_pick = stats[:, 0], stats[:, 1], stats[:, 2]
    global_max = jnp.max(all_max, axis=0)
    global_total = jnp.sum(all_total * jnp.exp(all_max - global_max[None, :]), axis=0)
    log_total = global_max + jnp.log(global_total)
    log_probs = logits - log_total[:, None]
    target_all = jnp.sum(all_pick, axis=0) - log_total
    target_logp = lax.dynamic_slice_in_dim(target_all, my_index * score_count, score_count, 0)
    return (layer_out, log_probs, target_logp)


def solution(mesh):
    parts, seq = mesh.shape["parts"], mesh.shape["seq"]
    devices = np.asarray(mesh.devices).reshape(parts, seq // CORES, CORES)
    fine = Mesh(devices, ("parts",) + SEQ)
    rows = ("parts",) + SEQ
    in_specs = (
        P(rows, None),
        P(rows, None),
        P(rows),
        P(rows, None),
        P(),
        P(SEQ, None),
        P(SEQ, None),
        P("parts"),
    )
    out_specs = (P(rows, None), P("parts", SEQ), P(rows))
    return jax.shard_map(local, mesh=fine, in_specs=in_specs, out_specs=out_specs, check_vma=False)
```

```python
import jax
import jax.numpy as jnp
import numpy as np
from jax import lax
from jax.sharding import Mesh
from jax.sharding import PartitionSpec as P

QUERY_HEADS = 16
KEY_VALUE_HEADS = 8
HEAD_SIZE = 128
ATTENTION_SPAN = 1024
SCORE_DEV = 4
SEG_LANES = 128
LANES = 128
CORES = 2
SEQ = ("chip", "core")


score_scale = 168.0 ** (-0.5)
masked_score = -1e30


def seq_count():
    return lax.axis_size("chip") * lax.axis_size("core")


def seq_index():
    return lax.axis_index("chip") * lax.axis_size("core") + lax.axis_index("core")


def forward_one(value):
    count = seq_count()
    return lax.ppermute(value, SEQ, [(source, source + 1) for source in range(count - 1)])


def swap_cores(value):
    return lax.ppermute(value, "core", [(0, 1), (1, 0)])


def gather_rows(value, radix=4):
    count = seq_count()
    me = seq_index()
    data = value[None]
    stride = 1
    while stride < count:
        digits = min(radix, count // stride)
        mine = (me // stride) % digits
        received = [data]
        for offset in range(1, digits):
            pairs = []
            for i in range(count):
                d = (i // stride) % digits
                pairs.append((i, i + (((d + offset) % digits) - d) * stride))
            received.append(lax.ppermute(data, SEQ, pairs))
        stacked = jnp.stack(received, 0)
        order = (mine - jnp.arange(digits)) % digits
        data = jnp.take(stacked, order, axis=0)
        data = data.reshape((digits * data.shape[1],) + data.shape[2:])
        stride *= digits
    return data.reshape((count * value.shape[0],) + value.shape[1:])


def in_core_order(mine, theirs, first):
    return jnp.where(first, jnp.concatenate([mine, theirs], 0), jnp.concatenate([theirs, mine], 0))


def shift_chips(value, chips):
    count = seq_count()
    step = chips * CORES
    return lax.ppermute(value, SEQ, [(s, s + step) for s in range(count - step)])


def across_pair(value, from_odd):
    count = seq_count()
    pairs = [(s, s ^ CORES) for s in range(count) if ((s // CORES) % 2 == 1) == from_odd]
    return lax.ppermute(value, SEQ, pairs)


def halo_window(own, kv_width, blocks, first_core):
    assert blocks == 4 * CORES
    odd = (lax.axis_index("chip") % 2) == 1
    back2 = shift_chips(own, 2)
    own_to_odd = across_pair(own, False)
    partner_own = swap_cores(own)
    back4 = shift_chips(back2, 2)
    back2_to_even = across_pair(back2, True)
    back2_to_odd = across_pair(back2, False)
    back4_to_even = across_pair(back4, True)
    back1 = jnp.where(odd, own_to_odd, back2_to_even)
    back3 = jnp.where(odd, back2_to_odd, back4_to_even)
    near = swap_cores(jnp.stack([back1, back2], 0))
    far = swap_cores(jnp.stack([back3, back4], 0))
    pieces = []
    for mine, theirs in ((back4, far[1]), (back3, far[0]), (back2, near[1]), (back1, near[0]), (own, partner_own)):
        pieces.append(in_core_order(mine, theirs, first_core))
    sequence = jnp.concatenate(pieces, 0)
    token_rows = own.shape[0]
    core = lax.axis_index("core")
    window = lax.dynamic_slice_in_dim(sequence, core * token_rows, (blocks + 1) * token_rows, 0)
    return window[:, :kv_width], window[:, kv_width].astype(jnp.int32)


def normalize(hidden, norm_gain):
    mean_square = jnp.mean(hidden * hidden, axis=1, keepdims=True)
    return (hidden * lax.rsqrt(mean_square + 1e-06) * norm_gain[None, :]).astype(jnp.bfloat16)


def local(
    queries, joined_keys_values, segment_ids, residual, norm_gain, out_proj, head_weight, next_ids
):
    token_rows = queries.shape[0]
    blocks = ATTENTION_SPAN // token_rows
    queries_per_group = QUERY_HEADS // KEY_VALUE_HEADS
    kv_width = joined_keys_values.shape[1]
    width = residual.shape[1]
    my_index = seq_index()
    core = lax.axis_index("core")
    first_core = core == 0
    first_row = my_index * token_rows

    full_proj = lax.all_gather(out_proj, SEQ, axis=0, tiled=True)
    score_count = SCORE_DEV
    stride = token_rows // score_count

    seg_cols = jnp.broadcast_to(segment_ids.astype(jnp.bfloat16)[:, None], (token_rows, SEG_LANES))
    own = jnp.concatenate([joined_keys_values, seg_cols], 1)
    key_value_pair, key_seg = halo_window(own, kv_width, blocks, first_core)
    residual_rows, key_value_pair = lax.optimization_barrier(
        (residual.reshape(score_count, stride, width)[:, stride - 1, :], key_value_pair)
    )
    scored_residual = gather_rows(residual_rows)
    count_of_keys = key_value_pair.shape[0]
    query_pos = first_row + jnp.arange(token_rows, dtype=jnp.int32)
    key_pos = first_row - blocks * token_rows + jnp.arange(count_of_keys, dtype=jnp.int32)
    allowed = (segment_ids[:, None] == key_seg[None, :]) & (key_pos[None, :] >= 0)
    allowed = (
        allowed
        & (key_pos[None, :] <= query_pos[:, None])
        & (key_pos[None, :] > query_pos[:, None] - ATTENTION_SPAN)
    )
    heads_for_queries = queries.reshape(token_rows, KEY_VALUE_HEADS, queries_per_group, HEAD_SIZE)
    heads_for_keys = key_value_pair[:, : KEY_VALUE_HEADS * HEAD_SIZE].reshape(
        count_of_keys, KEY_VALUE_HEADS, HEAD_SIZE
    )
    heads_for_values = key_value_pair[:, KEY_VALUE_HEADS * HEAD_SIZE :].reshape(
        count_of_keys, KEY_VALUE_HEADS, HEAD_SIZE
    )
    scores = (
        jnp.einsum(
            "qhgd,khd->hgqk", heads_for_queries, heads_for_keys, preferred_element_type=jnp.float32
        )
        * score_scale
    )
    scores = jnp.where(allowed[None, None, :, :], scores, masked_score)
    row_max = jnp.max(scores, axis=-1, keepdims=True)
    raised = jnp.exp(scores - row_max)
    weights = (raised / jnp.sum(raised, axis=-1, keepdims=True)).astype(jnp.bfloat16)
    context = jnp.einsum(
        "hgqk,khd->qhgd", weights, heads_for_values, preferred_element_type=jnp.float32
    )
    context = context.reshape(token_rows, QUERY_HEADS * HEAD_SIZE).astype(jnp.bfloat16)

    scored_context = gather_rows(context.reshape(score_count, stride, -1)[:, stride - 1, :])
    both = jnp.dot(
        jnp.concatenate([scored_context, context], 0), full_proj, preferred_element_type=jnp.float32
    )
    scored_total = scored_context.shape[0]
    picked = scored_residual.astype(jnp.float32) + both[:scored_total]
    normed = normalize(picked, norm_gain)
    projected = both[scored_total:]
    hidden = residual.astype(jnp.float32) + projected
    layer_out = hidden.astype(jnp.bfloat16)
    logits = lax.dot_general(
        normed,
        head_weight,
        (((1,), (1,)), ((), ())),
        preferred_element_type=jnp.float32,
    )
    vocab_width = head_weight.shape[0]
    local_ids = next_ids - my_index * vocab_width
    vocab_ids = jnp.arange(vocab_width, dtype=jnp.int32)
    shard_max = jnp.max(logits, axis=1)
    shard_total = jnp.sum(jnp.exp(logits - shard_max[:, None]), axis=1)
    shard_pick = jnp.sum(jnp.where(local_ids[:, None] == vocab_ids[None, :], logits, 0.0), axis=1)
    stats = gather_rows(jnp.stack([shard_max, shard_total, shard_pick], 0))
    stats = stats.reshape(-1, 3, shard_max.shape[0])
    all_max, all_total, all_pick = stats[:, 0], stats[:, 1], stats[:, 2]
    global_max = jnp.max(all_max, axis=0)
    global_total = jnp.sum(all_total * jnp.exp(all_max - global_max[None, :]), axis=0)
    log_total = global_max + jnp.log(global_total)
    log_probs = logits - log_total[:, None]
    target_all = jnp.sum(all_pick, axis=0) - log_total
    target_logp = lax.dynamic_slice_in_dim(target_all, my_index * score_count, score_count, 0)
    return (layer_out, log_probs, target_logp)


def solution(mesh):
    parts, seq = mesh.shape["parts"], mesh.shape["seq"]
    devices = np.asarray(mesh.devices).reshape(parts, seq // CORES, CORES)
    fine = Mesh(devices, ("parts",) + SEQ)
    rows = ("parts",) + SEQ
    in_specs = (
        P(rows, None),
        P(rows, None),
        P(rows),
        P(rows, None),
        P(),
        P(SEQ, None),
        P(SEQ, None),
        P("parts"),
    )
    out_specs = (P(rows, None), P("parts", SEQ), P(rows))
    return jax.shard_map(local, mesh=fine, in_specs=in_specs, out_specs=out_specs, check_vma=False)
```
